512 devices in a mesh: dp: 16 (over y, x_hi, core), tensor: 32 (over x_lo, z).
Axes of the slice: x: 4 (x_hi: 2, x_lo: 2; x = x_hi * 2 + x_lo), y: 4, z: 16, core: 2. Of those that a mesh axis runs over, the one named last changes fastest.
Arguments:
- loader_rows: bfloat16 [16, 32, 32, 4096], P('dp', 'tensor'), may hold values from -23 to 23
- row_counts: int32 [16, 32], P('dp', 'tensor'), may hold values from 0 to 32
- row_targets: int32 [16, 32, 32], P('dp', 'tensor'), may hold values from 0 to 255, as said below
- gate_weight: bfloat16 [4096, 16384], P('dp', 'tensor'), may hold values from -0.09375 to 0.09375
- up_weight: bfloat16 [4096, 16384], P('dp', 'tensor'), may hold values from -0.09375 to 0.09375
- down_weight: bfloat16 [16384, 4096], P('tensor'), may hold values from -0.046875 to 0.046875
Outputs:
- layer_out: bfloat16 [8192, 4096], P(('dp', 'tensor'))
The draws below stay inside these ranges and needn't reach their ends.
Inputs may be any that keep to these rules, and one draw needn't show every extreme that they name: `row_targets`: among the first row_counts[d, t] slots of replica d and tensor index t, a value v names row v % 16 of the rows of tensor index t on replica v // 16; over all replicas each such row is named exactly once, and no device names more than 2 rows of one replica. Slots past the count hold arbitrary values of the same range.
All inputs are finite; a program needn't handle non-finite values.
Results may differ from the reference program's by a relative error of at most 0.0095.
Values may be sent and summed in bfloat16 or wider, within the bound.
No kernel may reach another device: no remote copies, remote signals or barrier semaphores. Data moves between devices by JAX's collectives and lax.ppermute only.
A program may use at most 64 MiB of HBM per device.

```python
import math
import jax
import jax.numpy as jnp
from jax import lax

D = 4096
FF = 16384
ROWS_GRP = 512
ROWS_TP = 16
CAP = 2
SLOTS = 32
TOKENS = 8192
N_DP = 16
N_TENSOR = 32


def draw_plan(key):
    item_count = N_DP * CAP
    key_favored, key_bias, key_jitter, key_shuffle, key_filler = jax.random.split(jax.random.fold_in(key, 7), 5)
    key_common = jax.random.fold_in(key, 13)
    favored = jax.random.randint(key_favored, (N_TENSOR, N_DP), 0, N_DP).astype(jnp.int32)
    common_index = jax.random.randint(key_common, (), 0, N_TENSOR).astype(jnp.int32)
    common_row = jnp.arange(N_TENSOR, dtype=jnp.int32)[:, None] == common_index
    favored = jnp.where(common_row, jnp.broadcast_to(favored[:, :1], (N_TENSOR, N_DP)), favored).astype(jnp.int32)
    heavy_bias = jax.random.randint(key_bias, (N_TENSOR, 1, N_DP), 0, 2 ** 14).astype(jnp.int32)
    jitter = jax.random.randint(key_jitter, (N_TENSOR, N_DP, item_count), 0, 2 ** 14).astype(jnp.int32)
    item_index = jnp.arange(item_count, dtype=jnp.int32)
    source = item_index // CAP
    item_score = (jitter + jnp.repeat(heavy_bias, CAP, axis=2)) * item_count + item_index[None, None, :]
    item_score = jnp.where(source[None, None, :] == favored[:, :, None], item_index[None, None, :] - item_count, item_score)
    item_order = jnp.argsort(item_score, axis=2)
    slot_rank = jnp.argsort(item_order, axis=2).astype(jnp.int32)
    chosen = slot_rank < ROWS_TP
    is_live = chosen.reshape(N_TENSOR, N_DP, N_DP, CAP).transpose(0, 2, 1, 3).reshape(N_TENSOR, N_DP, item_count)
    target_row = jnp.arange(N_DP, dtype=jnp.int32)[None, :, None, None] * ROWS_TP + slot_rank.reshape(N_TENSOR, N_DP, N_DP, CAP)
    target_row = target_row.transpose(0, 2, 1, 3).reshape(N_TENSOR, N_DP, item_count)
    shuffle_key = jax.random.randint(key_shuffle, (N_TENSOR, N_DP, item_count), 0, 2 ** 14).astype(jnp.int32) * item_count + item_index[None, None, :]
    shuffle_key = jnp.where(is_live, shuffle_key, shuffle_key + 2 ** 24)
    shuffle_order = jnp.argsort(shuffle_key, axis=2)
    live_sorted = jnp.take_along_axis(is_live, shuffle_order, axis=2)
    target_sorted = jnp.take_along_axis(target_row, shuffle_order, axis=2)
    filler = jax.random.randint(key_filler, (N_TENSOR, N_DP, item_count), 0, N_DP * ROWS_TP).astype(jnp.int32)
    targets = jnp.where(live_sorted, target_sorted, filler).astype(jnp.int32)
    counts = jnp.sum(is_live.astype(jnp.int32), axis=2).astype(jnp.int32)
    return (counts.transpose(1, 0), targets.transpose(1, 0, 2))


def draw_row_counts(key, part):
    return draw_plan(key)[0]


def draw_row_targets(key, part):
    return draw_plan(key)[1]


def draw_loader_rows(key, part):
    key_base, key_rows, key_cols = jax.random.split(jax.random.fold_in(key, 11), 3)
    shape = (N_DP, N_TENSOR, SLOTS, D)
    base_draw = jnp.clip(jax.random.normal(key_base, shape, jnp.float32), -5.0, 5.0)
    row_scale = jnp.exp(jax.random.uniform(key_rows, (N_DP, N_TENSOR, SLOTS, 1), jnp.float32, math.log(0.3), math.log(3.0)))
    col_scale = jax.random.uniform(key_cols, (D,), jnp.float32, 0.5, 1.5)
    return (base_draw * row_scale * col_scale).astype(jnp.bfloat16)


def block_scale(stream_key, dims, pieces, least, largest):
    gain = 1.0
    for position, shards_of in pieces:
        steps = jax.random.uniform(jax.random.fold_in(jax.random.fold_in(stream_key, 6), position), (shards_of,), jnp.float32, least / len(pieces), largest / len(pieces))
        gain = gain * jnp.repeat(jnp.exp(steps), dims[position] // shards_of).reshape((-1,) + (1,) * (len(dims) - 1 - position))
    return gain


def normal_values(rng, shape, spread, limit, shards=(), kind=jnp.bfloat16):
    level = block_scale(rng, shape, shards, -0.22, 0.18) if shards else 1.0
    array = jax.random.normal(rng, shape, jnp.float32) * spread * level
    return jnp.minimum(jnp.maximum(array, -limit), limit).astype(kind)


def setup_inputs(seed: int = 0) -> dict:
    arg_keys = jax.random.split(jax.random.key(seed), 7)
    loader_rows = draw_loader_rows(jax.random.fold_in(arg_keys[6], 71), 0)
    row_counts = draw_row_counts(jax.random.fold_in(arg_keys[6], 71), 0)
    row_targets = draw_row_targets(jax.random.fold_in(arg_keys[6], 71), 0)
    gate_weight = normal_values(arg_keys[3], (D, FF), D ** -0.5, 0.09375, ((0, 16), (1, 32)))
    up_weight = normal_values(arg_keys[4], (D, FF), D ** -0.5, 0.09375, ((0, 16), (1, 32)))
    down_weight = normal_values(arg_keys[5], (FF, D), FF ** -0.5, 0.046875, ((0, 32),))
    return dict(loader_rows=loader_rows, row_counts=row_counts, row_targets=row_targets, gate_weight=gate_weight, up_weight=up_weight, down_weight=down_weight)


def reference(loader_rows, row_counts, row_targets, gate_weight, up_weight, down_weight):
    shard_rows = ROWS_GRP // N_TENSOR
    slot_index = jnp.arange(SLOTS, dtype=jnp.int32)
    is_live = slot_index[None, None, :] < row_counts[:, :, None]
    tensor_index = jnp.arange(N_TENSOR, dtype=jnp.int32)[None, :, None]
    where_to = row_targets // shard_rows * ROWS_GRP + tensor_index * shard_rows + row_targets % shard_rows
    live_values = jnp.where(is_live[..., None], loader_rows.astype(jnp.float32), jnp.float32(0.0))
    batch = jnp.zeros((TOKENS, D), jnp.float32).at[where_to.reshape(-1).astype(jnp.int32)].add(live_values.reshape(-1, D))
    batch = batch.astype(jnp.bfloat16)
    wide_batch = batch.astype(jnp.float32)
    normed = (wide_batch * lax.rsqrt(lax.optimization_barrier(jnp.mean(wide_batch * wide_batch, axis=1, keepdims=True)) + 1e-05)).astype(jnp.bfloat16)
    gate_act = jnp.dot(normed, gate_weight, preferred_element_type=jnp.float32)
    up_act = jnp.dot(normed, up_weight, preferred_element_type=jnp.float32)
    hidden = (jax.nn.silu(gate_act) * up_act).astype(jnp.bfloat16)
    block_width = FF // N_TENSOR
    hidden_blocks = hidden.reshape(TOKENS, N_TENSOR, block_width).transpose(1, 0, 2)
    down_blocks = down_weight.reshape(N_TENSOR, block_width, D)

    def add_block(total_sum, block_pair):
        block_term = jnp.dot(block_pair[0], block_pair[1], preferred_element_type=jnp.float32)
        block_term = lax.optimization_barrier(block_term.astype(jnp.bfloat16)).astype(jnp.float32)
        return (total_sum + block_term, None)
    total_sum, unused = lax.scan(add_block, jnp.zeros((TOKENS, D), jnp.float32), (hidden_blocks, down_blocks))
    return (wide_batch + total_sum).astype(jnp.bfloat16)
```

```python
import jax
import jax.numpy as jnp
from jax import lax
from jax.sharding import PartitionSpec as P

ROWS_GRP = 512
DP_SUB = (4, 2, 2)
TP_SUB = (2, 16)


def dp_perm(move):
    ny, nx, nc = DP_SUB
    pairs = []
    for y in range(ny):
        for x in range(nx):
            for c in range(nc):
                ty, tx, tc = move(y, x, c)
                pairs.append((y * nx * nc + x * nc + c, (ty % ny) * nx * nc + (tx % nx) * nc + tc % nc))
    return pairs


def tp_perm(move):
    nl, nz = TP_SUB
    pairs = []
    for l in range(nl):
        for z in range(nz):
            tl, tz = move(l, z)
            pairs.append((l * nz + z, (tl % nl) * nz + tz % nz))
    return pairs


DP_Y_FWD = dp_perm(lambda y, x, c: (y + 1, x, c))
DP_Y_BWD = dp_perm(lambda y, x, c: (y - 1, x, c))
DP_X_SWAP = dp_perm(lambda y, x, c: (y, x + 1, c))
DP_C_SWAP = dp_perm(lambda y, x, c: (y, x, c + 1))
TP_L_SWAP = tp_perm(lambda l, z: (l + 1, z))
TP_Z_FWD = tp_perm(lambda l, z: (l, z + 1))
TP_Z_BWD = tp_perm(lambda l, z: (l, z - 1))


def normalize(row_block):
    wide_rows = row_block.astype(jnp.float32)
    return (
        wide_rows * lax.rsqrt(jnp.mean(wide_rows * wide_rows, axis=1, keepdims=True) + 1e-05)
    ).astype(jnp.bfloat16)


def y_ring(chunks, key_of):
    out = dict(chunks)
    stacked = jnp.stack([chunks[k] for k in sorted(chunks)])
    keys = sorted(chunks)
    fwd = stacked
    for s in range(2):
        fwd = lax.ppermute(fwd, "dp", DP_Y_FWD)
        for i, k in enumerate(keys):
            out[key_of(k, DP_SUB[0] - 1 - s)] = fwd[i]
    bwd = lax.ppermute(stacked, "dp", DP_Y_BWD)
    for i, k in enumerate(keys):
        out[key_of(k, 1)] = bwd[i]
    return out


def swap(chunks, perm, key_of):
    out = dict(chunks)
    keys = sorted(chunks)
    got = lax.ppermute(jnp.stack([chunks[k] for k in keys]), "dp", perm)
    for i, k in enumerate(keys):
        out[key_of(k)] = got[i]
    return out


def gather_weight(piece, y_first):
    set_y = lambda k, v: (v, k[1], k[2])
    set_x = lambda k: (k[0], 1, k[2])
    set_c = lambda k: (k[0], k[1], 1)
    chunks = {(0, 0, 0): piece}
    if y_first:
        chunks = y_ring(chunks, set_y)
        chunks = swap(chunks, DP_X_SWAP, set_x)
    else:
        chunks = swap(chunks, DP_X_SWAP, set_x)
        chunks = y_ring(chunks, set_y)
    chunks = swap(chunks, DP_C_SWAP, set_c)
    return chunks


def per_device(loader_rows, row_counts, row_targets, gate_weight, up_weight, down_weight):
    dp_count = lax.axis_size("dp")
    tp_count = lax.axis_size("tensor")
    slot_rows = loader_rows[0, 0]
    slot_targets = row_targets[0, 0]
    live_count = row_counts[0, 0]
    slot_count = slot_rows.shape[0]
    feature_count = slot_rows.shape[1]
    per_peer = slot_count // dp_count
    shard_rows = ROWS_GRP // tp_count
    slot_index = jnp.arange(slot_count, dtype=jnp.int32)
    is_live = slot_index < live_count
    peer_index = slot_targets // shard_rows
    row_place = slot_targets % shard_rows
    peer_hot = (
        (peer_index[:, None] == jnp.arange(dp_count, dtype=jnp.int32)[None, :]) & is_live[:, None]
    ).astype(jnp.int32)
    earlier = jnp.cumsum(peer_hot, axis=0) - peer_hot
    slot_rank = jnp.sum(earlier * peer_hot, axis=1)
    send_slot = peer_index * per_peer + slot_rank
    pick_matrix = (send_slot[None, :] == slot_index[:, None]) & is_live[None, :]
    outgoing = jnp.dot(
        pick_matrix.astype(jnp.bfloat16), slot_rows, preferred_element_type=jnp.float32
    ).astype(jnp.bfloat16)
    out_place = jnp.sum(jnp.where(pick_matrix, row_place[None, :] + 1, 0), axis=1) - 1
    arrived, arrived_place = (
        lax.all_to_all(
            outgoing.reshape(dp_count, per_peer, feature_count),
            "dp",
            split_axis=0,
            concat_axis=0,
            tiled=True,
        ),
        lax.all_to_all(
            out_place.reshape(dp_count, per_peer), "dp", split_axis=0, concat_axis=0, tiled=True
        ),
    )
    land_matrix = (
        arrived_place.reshape(slot_count)[None, :]
        == jnp.arange(shard_rows, dtype=jnp.int32)[:, None]
    ).astype(jnp.bfloat16)
    local_batch = jnp.dot(
        land_matrix, arrived.reshape(slot_count, feature_count), preferred_element_type=jnp.float32
    ).astype(jnp.bfloat16)

    gate_chunks = gather_weight(gate_weight, True)
    up_chunks = gather_weight(up_weight, False)
    keys = sorted(gate_chunks)
    ny, nx, nc = DP_SUB
    me = lax.axis_index("dp")
    my_y, my_x, my_c = me // (nx * nc), (me // nc) % nx, me % nc
    piece_index = jnp.stack(
        [((my_y + k[0]) % ny) * nx * nc + ((my_x + k[1]) % nx) * nc + (my_c + k[2]) % nc for k in keys]
    ).astype(jnp.int32)
    gate_full = jnp.concatenate([gate_chunks[k] for k in keys], axis=0)
    up_full = jnp.concatenate([up_chunks[k] for k in keys], axis=0)

    nl, nz = TP_SUB
    travelling = normalize(local_batch)
    pair = jnp.stack([travelling, lax.ppermute(travelling, "tensor", TP_L_SWAP)])
    token_chunks = {0: pair}
    fwd = pair
    for s in range(nz // 2):
        fwd = lax.ppermute(fwd, "tensor", TP_Z_FWD)
        token_chunks[nz - 1 - s] = fwd
    bwd = pair
    for s in range(nz // 2 - 1):
        bwd = lax.ppermute(bwd, "tensor", TP_Z_BWD)
        token_chunks[s + 1] = bwd
    gathered = jnp.concatenate([token_chunks[k] for k in range(nz)], axis=0)
    row_total = gathered.shape[0] * gathered.shape[1]
    gathered = gathered.reshape(row_total, feature_count)
    piece_rows = gate_weight.shape[0]
    by_piece = gathered.reshape(row_total, dp_count, piece_rows)
    normed = jnp.take(by_piece, piece_index, axis=1).reshape(row_total, feature_count)

    gate_act = jnp.dot(normed, gate_full, preferred_element_type=jnp.float32)
    up_act = jnp.dot(normed, up_full, preferred_element_type=jnp.float32)
    hidden = (jax.nn.silu(gate_act) * up_act).astype(jnp.bfloat16)
    term = jnp.dot(hidden, down_weight, preferred_element_type=jnp.float32).astype(jnp.bfloat16)
    blocks = term.reshape(nz, nl, shard_rows, feature_count)

    fwd = blocks[nz // 2]
    for s in range(nz // 2):
        got = lax.ppermute(fwd, "tensor", TP_Z_FWD)
        if s < nz // 2 - 1:
            fwd = (got.astype(jnp.float32) + blocks[nz // 2 - 1 - s].astype(jnp.float32)).astype(jnp.bfloat16)
        else:
            fwd_total = got
    bwd = blocks[nz // 2 + 1]
    for s in range(nz // 2 - 1):
        got = lax.ppermute(bwd, "tensor", TP_Z_BWD)
        if s < nz // 2 - 2:
            bwd = (got.astype(jnp.float32) + blocks[nz // 2 + 2 + s].astype(jnp.float32)).astype(jnp.bfloat16)
        else:
            bwd_total = got
    column_sum = (
        fwd_total.astype(jnp.float32) + bwd_total.astype(jnp.float32) + blocks[0].astype(jnp.float32)
    )
    from_partner = lax.ppermute(column_sum[1].astype(jnp.bfloat16), "tensor", TP_L_SWAP)
    total = column_sum[0] + from_partner.astype(jnp.float32)
    return (local_batch.astype(jnp.float32) + total).astype(jnp.bfloat16)


def solution(mesh):
    placed = (
        P("dp", "tensor", None, None),
        P("dp", "tensor"),
        P("dp", "tensor", None),
        P("dp", "tensor"),
        P("dp", "tensor"),
        P("tensor", None),
    )
    return jax.shard_map(
        per_device, mesh=mesh, in_specs=placed, out_specs=P(("dp", "tensor"), None), check_vma=False
    )
```

```python
import jax
import jax.numpy as jnp
from jax import lax
from jax.sharding import PartitionSpec as P

ROWS_GRP = 512
DP_SUB = (4, 2, 2)
TP_SUB = (2, 16)


def dp_perm(move):
    ny, nx, nc = DP_SUB
    pairs = []
    for y in range(ny):
        for x in range(nx):
            for c in range(nc):
                ty, tx, tc = move(y, x, c)
                pairs.append((y * nx * nc + x * nc + c, (ty % ny) * nx * nc + (tx % nx) * nc + tc % nc))
    return pairs


def tp_perm(move):
    nl, nz = TP_SUB
    pairs = []
    for l in range(nl):
        for z in range(nz):
            tl, tz = move(l, z)
            pairs.append((l * nz + z, (tl % nl) * nz + tz % nz))
    return pairs


DP_Y_FWD = dp_perm(lambda y, x, c: (y + 1, x, c))
DP_Y_BWD = dp_perm(lambda y, x, c: (y - 1, x, c))
DP_X_SWAP = dp_perm(lambda y, x, c: (y, x + 1, c))
DP_C_SWAP = dp_perm(lambda y, x, c: (y, x, c + 1))
TP_L_SWAP = tp_perm(lambda l, z: (l + 1, z))
TP_Z_FWD = tp_perm(lambda l, z: (l, z + 1))
TP_Z_BWD = tp_perm(lambda l, z: (l, z - 1))


def normalize(row_block):
    wide_rows = row_block.astype(jnp.float32)
    return (
        wide_rows * lax.rsqrt(jnp.mean(wide_rows * wide_rows, axis=1, keepdims=True) + 1e-05)
    ).astype(jnp.bfloat16)


def gather_pieces(piece):
    ny = DP_SUB[0]
    own = piece[None]
    across = lax.ppermute(own, "dp", DP_X_SWAP)
    pair = jnp.concatenate([own, across])
    pair_keys = [(0, 0, 0), (0, 1, 0)]
    fwd1 = lax.ppermute(pair, "dp", DP_Y_FWD)
    fwd2 = lax.ppermute(fwd1, "dp", DP_Y_FWD)
    bwd1 = lax.ppermute(pair, "dp", DP_Y_BWD)
    shift = lambda keys, dy: [((k[0] + dy) % ny, k[1], k[2]) for k in keys]
    chip = jnp.concatenate([pair, fwd1, fwd2, bwd1])
    chip_keys = pair_keys + shift(pair_keys, ny - 1) + shift(pair_keys, ny - 2) + shift(pair_keys, 1)
    other_core = lax.ppermute(chip, "dp", DP_C_SWAP)
    return [
        ([(0, 0, 0)], own),
        ([(0, 1, 0)], across),
        (shift(pair_keys, ny - 1), fwd1),
        (shift(pair_keys, ny - 2), fwd2),
        (shift(pair_keys, 1), bwd1),
        ([(k[0], k[1], 1) for k in chip_keys], other_core),
    ]


def per_device(loader_rows, row_counts, row_targets, gate_weight, up_weight, down_weight):
    dp_count = lax.axis_size("dp")
    tp_count = lax.axis_size("tensor")
    slot_rows = loader_rows[0, 0]
    slot_targets = row_targets[0, 0]
    live_count = row_counts[0, 0]
    slot_count = slot_rows.shape[0]
    feature_count = slot_rows.shape[1]
    per_peer = slot_count // dp_count
    shard_rows = ROWS_GRP // tp_count
    slot_index = jnp.arange(slot_count, dtype=jnp.int32)
    is_live = slot_index < live_count
    peer_index = slot_targets // shard_rows
    row_place = slot_targets % shard_rows
    peer_hot = (
        (peer_index[:, None] == jnp.arange(dp_count, dtype=jnp.int32)[None, :]) & is_live[:, None]
    ).astype(jnp.int32)
    earlier = jnp.cumsum(peer_hot, axis=0) - peer_hot
    slot_rank = jnp.sum(earlier * peer_hot, axis=1)
    send_slot = peer_index * per_peer + slot_rank
    pick_matrix = (send_slot[None, :] == slot_index[:, None]) & is_live[None, :]
    outgoing = jnp.dot(
        pick_matrix.astype(jnp.bfloat16), slot_rows, preferred_element_type=jnp.float32
    ).astype(jnp.bfloat16)
    out_place = jnp.sum(jnp.where(pick_matrix, row_place[None, :] + 1, 0), axis=1) - 1
    place_cols = jnp.broadcast_to(out_place.astype(jnp.bfloat16)[:, None], (slot_count, 128))
    arrived = lax.all_to_all(
        jnp.concatenate([outgoing, place_cols], axis=1).reshape(dp_count, per_peer, feature_count + 128),
        "dp",
        split_axis=0,
        concat_axis=0,
        tiled=True,
    ).reshape(slot_count, feature_count + 128)
    arrived_place = arrived[:, feature_count].astype(jnp.int32)
    land_matrix = (
        arrived_place[None, :] == jnp.arange(shard_rows, dtype=jnp.int32)[:, None]
    ).astype(jnp.bfloat16)
    local_batch = jnp.dot(
        land_matrix, arrived[:, :feature_count], preferred_element_type=jnp.float32
    ).astype(jnp.bfloat16)

    ff_cols = gate_weight.shape[1]
    piece_rows = gate_weight.shape[0]
    buffers = gather_pieces(jnp.concatenate([gate_weight, up_weight], axis=1))
    keys = [k for ks, _ in buffers for k in ks]
    ny, nx, nc = DP_SUB
    me = lax.axis_index("dp")
    my_y, my_x, my_c = me // (nx * nc), (me // nc) % nx, me % nc
    piece_index = jnp.stack(
        [((my_y + k[0]) % ny) * nx * nc + ((my_x + k[1]) % nx) * nc + (my_c + k[2]) % nc for k in keys]
    ).astype(jnp.int32)

    nl, nz = TP_SUB
    travelling = normalize(local_batch)
    travelling = jnp.take(
        travelling.reshape(shard_rows, dp_count, piece_rows), piece_index, axis=1
    ).reshape(shard_rows, feature_count)
    pair = jnp.stack([travelling, lax.ppermute(travelling, "tensor", TP_L_SWAP)])
    token_chunks = {0: pair}
    fwd = pair
    for s in range(nz // 2):
        fwd = lax.ppermute(fwd, "tensor", TP_Z_FWD)
        token_chunks[nz - 1 - s] = fwd
    bwd = pair
    for s in range(nz // 2 - 1):
        bwd = lax.ppermute(bwd, "tensor", TP_Z_BWD)
        token_chunks[s + 1] = bwd
    gathered = jnp.concatenate([token_chunks[k] for k in range(nz)], axis=0)
    row_total = gathered.shape[0] * gathered.shape[1]
    normed = gathered.reshape(row_total, feature_count)

    act = None
    col = 0
    for ks, buf in buffers:
        width = len(ks) * piece_rows
        part = jnp.dot(
            normed[:, col : col + width],
            buf.reshape(width, 2 * ff_cols),
            preferred_element_type=jnp.float32,
        )
        act = part if act is None else act + part
        col += width
    gate_act = act[:, :ff_cols]
    up_act = act[:, ff_cols:]
    hidden = (jax.nn.silu(gate_act) * up_act).astype(jnp.bfloat16)
    term = jnp.dot(hidden, down_weight, preferred_element_type=jnp.float32).astype(jnp.bfloat16)
    blocks = term.reshape(nz, nl, shard_rows, feature_count)

    fwd = blocks[nz // 2]
    for s in range(nz // 2):
        got = lax.ppermute(fwd, "tensor", TP_Z_FWD)
        if s < nz // 2 - 1:
            fwd = (got.astype(jnp.float32) + blocks[nz // 2 - 1 - s].astype(jnp.float32)).astype(jnp.bfloat16)
        else:
            fwd_total = got
    bwd = blocks[nz // 2 + 1]
    for s in range(nz // 2 - 1):
        got = lax.ppermute(bwd, "tensor", TP_Z_BWD)
        if s < nz // 2 - 2:
            bwd = (got.astype(jnp.float32) + blocks[nz // 2 + 2 + s].astype(jnp.float32)).astype(jnp.bfloat16)
        else:
            bwd_total = got
    column_sum = (
        fwd_total.astype(jnp.float32) + bwd_total.astype(jnp.float32) + blocks[0].astype(jnp.float32)
    )
    from_partner = lax.ppermute(column_sum[1].astype(jnp.bfloat16), "tensor", TP_L_SWAP)
    total = column_sum[0] + from_partner.astype(jnp.float32)
    return (local_batch.astype(jnp.float32) + total).astype(jnp.bfloat16)


def solution(mesh):
    placed = (
        P("dp", "tensor", None, None),
        P("dp", "tensor"),
        P("dp", "tensor", None),
        P("dp", "tensor"),
        P("dp", "tensor"),
        P("tensor", None),
    )
    return jax.shard_map(
        per_device, mesh=mesh, in_specs=placed, out_specs=P(("dp", "tensor"), None), check_vma=False
    )
```

```python
import jax
import jax.numpy as jnp
from jax import lax
from jax.sharding import PartitionSpec as P

ROWS_GRP = 512
DP_SUB = (4, 2, 2)
TP_SUB = (2, 16)
SPLIT_COLS = 2688


def dp_perm(move):
    ny, nx, nc = DP_SUB
    pairs = []
    for y in range(ny):
        for x in range(nx):
            for c in range(nc):
                ty, tx, tc = move(y, x, c)
                pairs.append((y * nx * nc + x * nc + c, (ty % ny) * nx * nc + (tx % nx) * nc + tc % nc))
    return pairs


def tp_perm(move):
    nl, nz = TP_SUB
    pairs = []
    for l in range(nl):
        for z in range(nz):
            tl, tz = move(l, z)
            pairs.append((l * nz + z, (tl % nl) * nz + tz % nz))
    return pairs


DP_Y_FWD = dp_perm(lambda y, x, c: (y + 1, x, c))
DP_Y_BWD = dp_perm(lambda y, x, c: (y - 1, x, c))
DP_X_SWAP = dp_perm(lambda y, x, c: (y, x + 1, c))
DP_C_SWAP = dp_perm(lambda y, x, c: (y, x, c + 1))
TP_L_SWAP = tp_perm(lambda l, z: (l + 1, z))
TP_Z_FWD = tp_perm(lambda l, z: (l, z + 1))
TP_Z_BWD = tp_perm(lambda l, z: (l, z - 1))


def normalize(row_block):
    wide_rows = row_block.astype(jnp.float32)
    return (
        wide_rows * lax.rsqrt(jnp.mean(wide_rows * wide_rows, axis=1, keepdims=True) + 1e-05)
    ).astype(jnp.bfloat16)


def gather_pieces(piece):
    ny = DP_SUB[0]
    own = piece[None]
    across = lax.ppermute(own, "dp", DP_X_SWAP)
    pair = jnp.concatenate([own, across])
    pair_keys = [(0, 0, 0), (0, 1, 0)]
    fwd1 = lax.ppermute(pair, "dp", DP_Y_FWD)
    fwd2 = lax.ppermute(fwd1, "dp", DP_Y_FWD)
    bwd1 = lax.ppermute(pair, "dp", DP_Y_BWD)
    shift = lambda keys, dy: [((k[0] + dy) % ny, k[1], k[2]) for k in keys]
    chip = jnp.concatenate([pair, fwd1, fwd2, bwd1])
    chip_keys = pair_keys + shift(pair_keys, ny - 1) + shift(pair_keys, ny - 2) + shift(pair_keys, 1)
    other_core = lax.ppermute(chip, "dp", DP_C_SWAP)
    return [
        ([(0, 0, 0)], own),
        ([(0, 1, 0)], across),
        (shift(pair_keys, ny - 1), fwd1),
        (shift(pair_keys, ny - 2), fwd2),
        (shift(pair_keys, 1), bwd1),
        ([(k[0], k[1], 1) for k in chip_keys], other_core),
    ]


def per_device(loader_rows, row_counts, row_targets, gate_weight, up_weight, down_weight):
    dp_count = lax.axis_size("dp")
    tp_count = lax.axis_size("tensor")
    slot_rows = loader_rows[0, 0]
    slot_targets = row_targets[0, 0]
    live_count = row_counts[0, 0]
    slot_count = slot_rows.shape[0]
    feature_count = slot_rows.shape[1]
    per_peer = slot_count // dp_count
    shard_rows = ROWS_GRP // tp_count
    slot_index = jnp.arange(slot_count, dtype=jnp.int32)
    is_live = slot_index < live_count
    peer_index = slot_targets // shard_rows
    row_place = slot_targets % shard_rows
    peer_hot = (
        (peer_index[:, None] == jnp.arange(dp_count, dtype=jnp.int32)[None, :]) & is_live[:, None]
    ).astype(jnp.int32)
    earlier = jnp.cumsum(peer_hot, axis=0) - peer_hot
    slot_rank = jnp.sum(earlier * peer_hot, axis=1)
    send_slot = peer_index * per_peer + slot_rank
    pick_matrix = (send_slot[None, :] == slot_index[:, None]) & is_live[None, :]
    outgoing = jnp.dot(
        pick_matrix.astype(jnp.bfloat16), slot_rows, preferred_element_type=jnp.float32
    ).astype(jnp.bfloat16)
    out_place = jnp.sum(jnp.where(pick_matrix, row_place[None, :] + 1, 0), axis=1) - 1
    place_cols = jnp.broadcast_to(out_place.astype(jnp.bfloat16)[:, None], (slot_count, 128))
    arrived = lax.all_to_all(
        jnp.concatenate([outgoing, place_cols], axis=1).reshape(dp_count, per_peer, feature_count + 128),
        "dp",
        split_axis=0,
        concat_axis=0,
        tiled=True,
    ).reshape(slot_count, feature_count + 128)
    arrived_place = arrived[:, feature_count].astype(jnp.int32)
    land_matrix = (
        arrived_place[None, :] == jnp.arange(shard_rows, dtype=jnp.int32)[:, None]
    ).astype(jnp.bfloat16)
    local_batch = jnp.dot(
        land_matrix, arrived[:, :feature_count], preferred_element_type=jnp.float32
    ).astype(jnp.bfloat16)

    ff_cols = gate_weight.shape[1]
    piece_rows = gate_weight.shape[0]
    buffers = gather_pieces(jnp.concatenate([gate_weight, up_weight], axis=1))
    keys = [k for ks, _ in buffers for k in ks]
    ny, nx, nc = DP_SUB
    me = lax.axis_index("dp")
    my_y, my_x, my_c = me // (nx * nc), (me // nc) % nx, me % nc
    piece_index = jnp.stack(
        [((my_y + k[0]) % ny) * nx * nc + ((my_x + k[1]) % nx) * nc + (my_c + k[2]) % nc for k in keys]
    ).astype(jnp.int32)

    nl, nz = TP_SUB
    travelling = normalize(local_batch)
    travelling = jnp.take(
        travelling.reshape(shard_rows, dp_count, piece_rows), piece_index, axis=1
    ).reshape(shard_rows, feature_count)
    cut = SPLIT_COLS
    rest = feature_count - cut
    pack = lambda p, q: jnp.concatenate([p, q[0], q[1]], axis=1)
    unpack = lambda v: (v[:, :cut], jnp.stack([v[:, cut : cut + rest], v[:, cut + rest :]]))
    partner = lax.ppermute(travelling, "tensor", TP_L_SWAP)
    col_p = {0: travelling[:, :cut]}
    far_p = {0: partner[:, :cut]}
    q_pairs = {0: jnp.stack([travelling[:, cut:], partner[:, cut:]])}
    fwd = pack(col_p[0], q_pairs[0])
    bwd = fwd
    pending = []
    for s in range(nz // 2):
        if pending:
            crossed = lax.ppermute(jnp.stack([col_p[k] for k in pending]), "tensor", TP_L_SWAP)
            for i, k in enumerate(pending):
                far_p[k] = crossed[i]
        pending = []
        fwd = lax.ppermute(fwd, "tensor", TP_Z_FWD)
        col_p[nz - 1 - s], q_pairs[nz - 1 - s] = unpack(fwd)
        pending.append(nz - 1 - s)
        if s < nz // 2 - 1:
            bwd = lax.ppermute(bwd, "tensor", TP_Z_BWD)
            col_p[s + 1], q_pairs[s + 1] = unpack(bwd)
            pending.append(s + 1)
    crossed = lax.ppermute(jnp.stack([col_p[k] for k in pending]), "tensor", TP_L_SWAP)
    for i, k in enumerate(pending):
        far_p[k] = crossed[i]
    gathered = jnp.stack(
        [
            jnp.stack(
                [
                    jnp.concatenate([col_p[k], q_pairs[k][0]], axis=1),
                    jnp.concatenate([far_p[k], q_pairs[k][1]], axis=1),
                ]
            )
            for k in range(nz)
        ]
    )
    row_total = nz * nl * shard_rows
    normed = gathered.reshape(row_total, feature_count)

    act = None
    col = 0
    for ks, buf in buffers:
        width = len(ks) * piece_rows
        part = jnp.dot(
            normed[:, col : col + width],
            buf.reshape(width, 2 * ff_cols),
            preferred_element_type=jnp.float32,
        )
        act = part if act is None else act + part
        col += width
    gate_act = act[:, :ff_cols]
    up_act = act[:, ff_cols:]
    hidden = (jax.nn.silu(gate_act) * up_act).astype(jnp.bfloat16)
    term = jnp.dot(hidden, down_weight, preferred_element_type=jnp.float32).astype(jnp.bfloat16)
    blocks = term.reshape(nz, nl, shard_rows, feature_count)

    f32 = lambda v: v.astype(jnp.float32)
    bf16 = lambda v: v.astype(jnp.bfloat16)
    head = blocks[..., :cut]
    tail = blocks[..., cut:]
    col_sum = {}

    def cross_reduce(ks):
        got = lax.ppermute(jnp.stack([head[k, 1] for k in ks]), "tensor", TP_L_SWAP)
        for i, k in enumerate(ks):
            col_sum[k] = f32(head[k, 0]) + f32(got[i])

    cross_reduce([nz // 2, nz // 2 + 1, 0])
    fwd = pack(bf16(col_sum[nz // 2]), tail[nz // 2])
    bwd = pack(bf16(col_sum[nz // 2 + 1]), tail[nz // 2 + 1])
    for s in range(nz // 2):
        ks = []
        if s < nz // 2 - 1:
            ks.append(nz // 2 - 1 - s)
        if s < nz // 2 - 2:
            ks.append(nz // 2 + 2 + s)
        if ks:
            cross_reduce(ks)
        got = lax.ppermute(fwd, "tensor", TP_Z_FWD)
        if s < nz // 2 - 1:
            k = nz // 2 - 1 - s
            p, q = unpack(got)
            fwd = pack(bf16(f32(p) + col_sum[k]), bf16(f32(q) + f32(tail[k])))
        else:
            fwd_total = got
        if s < nz // 2 - 1:
            got = lax.ppermute(bwd, "tensor", TP_Z_BWD)
            if s < nz // 2 - 2:
                k = nz // 2 + 2 + s
                p, q = unpack(got)
                bwd = pack(bf16(f32(p) + col_sum[k]), bf16(f32(q) + f32(tail[k])))
            else:
                bwd_total = got
    f_p, f_q = unpack(fwd_total)
    b_p, b_q = unpack(bwd_total)
    total_head = f32(f_p) + f32(b_p) + col_sum[0]
    tail_sum = f32(f_q) + f32(b_q) + f32(tail[0])
    from_partner = lax.ppermute(bf16(tail_sum[1]), "tensor", TP_L_SWAP)
    total = jnp.concatenate([total_head, tail_sum[0] + f32(from_partner)], axis=1)
    return (local_batch.astype(jnp.float32) + total).astype(jnp.bfloat16)


def solution(mesh):
    placed = (
        P("dp", "tensor", None, None),
        P("dp", "tensor"),
        P("dp", "tensor", None),
        P("dp", "tensor"),
        P("dp", "tensor"),
        P("tensor", None),
    )
    return jax.shard_map(
        per_device, mesh=mesh, in_specs=placed, out_specs=P(("dp", "tensor"), None), check_vma=False
    )
```

```python
import jax
import jax.numpy as jnp
from jax import lax
from jax.sharding import PartitionSpec as P

ROWS_GRP = 512
DP_SUB = (4, 2, 2)
TP_SUB = (2, 16)


def dp_perm(move):
    ny, nx, nc = DP_SUB
    pairs = []
    for y in range(ny):
        for x in range(nx):
            for c in range(nc):
                ty, tx, tc = move(y, x, c)
                pairs.append((y * nx * nc + x * nc + c, (ty % ny) * nx * nc + (tx % nx) * nc + tc % nc))
    return pairs


def tp_perm(move):
    nl, nz = TP_SUB
    pairs = []
    for l in range(nl):
        for z in range(nz):
            tl, tz = move(l, z)
            pairs.append((l * nz + z, (tl % nl) * nz + tz % nz))
    return pairs


DP_Y_FWD = dp_perm(lambda y, x, c: (y + 1, x, c))
DP_Y_BWD = dp_perm(lambda y, x, c: (y - 1, x, c))
DP_X_SWAP = dp_perm(lambda y, x, c: (y, x + 1, c))
DP_C_SWAP = dp_perm(lambda y, x, c: (y, x, c + 1))
TP_L_SWAP = tp_perm(lambda l, z: (l + 1, z))
TP_Z_FWD = tp_perm(lambda l, z: (l, z + 1))
TP_Z_BWD = tp_perm(lambda l, z: (l, z - 1))


def normalize(row_block):
    wide_rows = row_block.astype(jnp.float32)
    return (
        wide_rows * lax.rsqrt(jnp.mean(wide_rows * wide_rows, axis=1, keepdims=True) + 1e-05)
    ).astype(jnp.bfloat16)


def gather_pieces(piece):
    ny = DP_SUB[0]
    own = piece[None]
    across = lax.ppermute(own, "dp", DP_X_SWAP)
    pair = jnp.concatenate([own, across])
    pair_keys = [(0, 0, 0), (0, 1, 0)]
    fwd1 = lax.ppermute(pair, "dp", DP_Y_FWD)
    fwd2 = lax.ppermute(fwd1, "dp", DP_Y_FWD)
    bwd1 = lax.ppermute(pair, "dp", DP_Y_BWD)
    shift = lambda keys, dy: [((k[0] + dy) % ny, k[1], k[2]) for k in keys]
    chip = jnp.concatenate([pair, fwd1, fwd2, bwd1])
    chip_keys = pair_keys + shift(pair_keys, ny - 1) + shift(pair_keys, ny - 2) + shift(pair_keys, 1)
    other_core = lax.ppermute(chip, "dp", DP_C_SWAP)
    return [
        ([(0, 0, 0)], own),
        ([(0, 1, 0)], across),
        (shift(pair_keys, ny - 1), fwd1),
        (shift(pair_keys, ny - 2), fwd2),
        (shift(pair_keys, 1), bwd1),
        ([(k[0], k[1], 1) for k in chip_keys], other_core),
    ]


def per_device(loader_rows, row_counts, row_targets, gate_weight, up_weight, down_weight):
    dp_count = lax.axis_size("dp")
    tp_count = lax.axis_size("tensor")
    slot_rows = loader_rows[0, 0]
    slot_targets = row_targets[0, 0]
    live_count = row_counts[0, 0]
    slot_count = slot_rows.shape[0]
    feature_count = slot_rows.shape[1]
    per_peer = slot_count // dp_count
    shard_rows = ROWS_GRP // tp_count
    slot_index = jnp.arange(slot_count, dtype=jnp.int32)
    is_live = slot_index < live_count
    peer_index = slot_targets // shard_rows
    row_place = slot_targets % shard_rows
    peer_hot = (
        (peer_index[:, None] == jnp.arange(dp_count, dtype=jnp.int32)[None, :]) & is_live[:, None]
    ).astype(jnp.int32)
    earlier = jnp.cumsum(peer_hot, axis=0) - peer_hot
    slot_rank = jnp.sum(earlier * peer_hot, axis=1)
    send_slot = peer_index * per_peer + slot_rank
    pick_matrix = (send_slot[None, :] == slot_index[:, None]) & is_live[None, :]
    outgoing = jnp.dot(
        pick_matrix.astype(jnp.bfloat16), slot_rows, preferred_element_type=jnp.float32
    ).astype(jnp.bfloat16)
    out_place = jnp.sum(jnp.where(pick_matrix, row_place[None, :] + 1, 0), axis=1) - 1
    place_cols = jnp.broadcast_to(out_place.astype(jnp.bfloat16)[:, None], (slot_count, 128))
    arrived = lax.all_to_all(
        jnp.concatenate([outgoing, place_cols], axis=1).reshape(dp_count, per_peer, feature_count + 128),
        "dp",
        split_axis=0,
        concat_axis=0,
        tiled=True,
    ).reshape(slot_count, feature_count + 128)
    arrived_place = arrived[:, feature_count].astype(jnp.int32)
    land_matrix = (
        arrived_place[None, :] == jnp.arange(shard_rows, dtype=jnp.int32)[:, None]
    ).astype(jnp.bfloat16)
    local_batch = jnp.dot(
        land_matrix, arrived[:, :feature_count], preferred_element_type=jnp.float32
    ).astype(jnp.bfloat16)

    ff_cols = gate_weight.shape[1]
    piece_rows = gate_weight.shape[0]
    own = jnp.concatenate([gate_weight, up_weight], axis=1)[None]
    across = lax.ppermute(own, "dp", DP_X_SWAP)
    pair_keys = [(0, 0, 0), (0, 1, 0)]
    shift = lambda ks, dy: [((k[0] + dy) % DP_SUB[0], k[1], k[2]) for k in ks]
    keys = (
        [(0, 0, 0), (0, 1, 0)]
        + shift(pair_keys, DP_SUB[0] - 1)
        + shift(pair_keys, DP_SUB[0] - 2)
        + shift(pair_keys, 1)
    )
    keys = keys + [(k[0], k[1], 1) for k in keys]
    ny, nx, nc = DP_SUB
    me = lax.axis_index("dp")
    my_y, my_x, my_c = me // (nx * nc), (me // nc) % nx, me % nc
    piece_index = jnp.stack(
        [((my_y + k[0]) % ny) * nx * nc + ((my_x + k[1]) % nx) * nc + (my_c + k[2]) % nc for k in keys]
    ).astype(jnp.int32)

    nl, nz = TP_SUB
    travelling = normalize(local_batch)
    travelling = jnp.take(
        travelling.reshape(shard_rows, dp_count, piece_rows), piece_index, axis=1
    ).reshape(shard_rows, feature_count)
    pair = jnp.stack([travelling, lax.ppermute(travelling, "tensor", TP_L_SWAP)])
    token_chunks = {0: pair}
    fwd = pair
    bwd = pair
    for s in range(nz // 2):
        if s == 1:
            fwd, bwd, across = lax.optimization_barrier((fwd, bwd, across))
            w_pair = jnp.concatenate([own, across])
            w_fwd1 = lax.ppermute(w_pair, "dp", DP_Y_FWD)
            w_bwd1 = lax.ppermute(w_pair, "dp", DP_Y_BWD)
        if s == 4:
            fwd, bwd, w_fwd1, w_bwd1 = lax.optimization_barrier((fwd, bwd, w_fwd1, w_bwd1))
            w_fwd2 = lax.ppermute(w_fwd1, "dp", DP_Y_FWD)
        if s == 6:
            fwd, bwd, w_fwd2 = lax.optimization_barrier((fwd, bwd, w_fwd2))
            w_chip = jnp.concatenate([w_pair, w_fwd1, w_fwd2, w_bwd1])
            w_other = lax.ppermute(w_chip, "dp", DP_C_SWAP)
        fwd = lax.ppermute(fwd, "tensor", TP_Z_FWD)
        token_chunks[nz - 1 - s] = fwd
        if s < nz // 2 - 1:
            bwd = lax.ppermute(bwd, "tensor", TP_Z_BWD)
            token_chunks[s + 1] = bwd
    buffers = [
        ([(0, 0, 0), (0, 1, 0)], w_pair),
        ([None] * 2, w_fwd1),
        ([None] * 2, w_fwd2),
        ([None] * 2, w_bwd1),
        ([None] * 8, w_other),
    ]
    gathered = jnp.concatenate([token_chunks[k] for k in range(nz)], axis=0)
    row_total = gathered.shape[0] * gathered.shape[1]
    normed = gathered.reshape(row_total, feature_count)

    act = None
    col = 0
    for ks, buf in buffers:
        width = len(ks) * piece_rows
        part = jnp.dot(
            normed[:, col : col + width],
            buf.reshape(width, 2 * ff_cols),
            preferred_element_type=jnp.float32,
        )
        act = part if act is None else act + part
        col += width
    gate_act = act[:, :ff_cols]
    up_act = act[:, ff_cols:]
    hidden = (jax.nn.silu(gate_act) * up_act).astype(jnp.bfloat16)
    term = jnp.dot(hidden, down_weight, preferred_element_type=jnp.float32).astype(jnp.bfloat16)
    blocks = term.reshape(nz, nl, shard_rows, feature_count)

    fwd = blocks[nz // 2]
    for s in range(nz // 2):
        got = lax.ppermute(fwd, "tensor", TP_Z_FWD)
        if s < nz // 2 - 1:
            fwd = (got.astype(jnp.float32) + blocks[nz // 2 - 1 - s].astype(jnp.float32)).astype(jnp.bfloat16)
        else:
            fwd_total = got
    bwd = blocks[nz // 2 + 1]
    for s in range(nz // 2 - 1):
        got = lax.ppermute(bwd, "tensor", TP_Z_BWD)
        if s < nz // 2 - 2:
            bwd = (got.astype(jnp.float32) + blocks[nz // 2 + 2 + s].astype(jnp.float32)).astype(jnp.bfloat16)
        else:
            bwd_total = got
    column_sum = (
        fwd_total.astype(jnp.float32) + bwd_total.astype(jnp.float32) + blocks[0].astype(jnp.float32)
    )
    from_partner = lax.ppermute(column_sum[1].astype(jnp.bfloat16), "tensor", TP_L_SWAP)
    total = column_sum[0] + from_partner.astype(jnp.float32)
    return (local_batch.astype(jnp.float32) + total).astype(jnp.bfloat16)


def solution(mesh):
    placed = (
        P("dp", "tensor", None, None),
        P("dp", "tensor"),
        P("dp", "tensor", None),
        P("dp", "tensor"),
        P("dp", "tensor"),
        P("tensor", None),
    )
    return jax.shard_map(
        per_device, mesh=mesh, in_specs=placed, out_specs=P(("dp", "tensor"), None), check_vma=False
    )
```

```python
import jax
import jax.numpy as jnp
from jax import lax
from jax.sharding import PartitionSpec as P

ROWS_GRP = 512
DP_SUB = (4, 2, 2)
TP_SUB = (2, 16)


def dp_perm(move):
    ny, nx, nc = DP_SUB
    pairs = []
    for y in range(ny):
        for x in range(nx):
            for c in range(nc):
                ty, tx, tc = move(y, x, c)
                pairs.append((y * nx * nc + x * nc + c, (ty % ny) * nx * nc + (tx % nx) * nc + tc % nc))
    return pairs


def tp_perm(move):
    nl, nz = TP_SUB
    pairs = []
    for l in range(nl):
        for z in range(nz):
            tl, tz = move(l, z)
            pairs.append((l * nz + z, (tl % nl) * nz + tz % nz))
    return pairs


DP_Y_FWD = dp_perm(lambda y, x, c: (y + 1, x, c))
DP_Y_BWD = dp_perm(lambda y, x, c: (y - 1, x, c))
DP_X_SWAP = dp_perm(lambda y, x, c: (y, x + 1, c))
DP_C_SWAP = dp_perm(lambda y, x, c: (y, x, c + 1))
TP_L_SWAP = tp_perm(lambda l, z: (l + 1, z))
TP_Z_FWD = tp_perm(lambda l, z: (l, z + 1))
TP_Z_BWD = tp_perm(lambda l, z: (l, z - 1))


def split_perm(cores):
    n_tp = TP_SUB[0] * TP_SUB[1]
    n_dp = DP_SUB[0] * DP_SUB[1] * DP_SUB[2]
    fwd = dict(TP_Z_FWD)
    bwd = dict(TP_Z_BWD)
    return [
        (d * n_tp + t, d * n_tp + (fwd[t] if d % 2 == 0 else bwd[t]))
        for d in range(n_dp)
        for t in range(n_tp)
        if d % 2 in cores
    ]


SPLIT_BOTH = split_perm((0, 1))
SPLIT_FWD_ONLY = split_perm((0,))


def normalize(row_block):
    wide_rows = row_block.astype(jnp.float32)
    return (
        wide_rows * lax.rsqrt(jnp.mean(wide_rows * wide_rows, axis=1, keepdims=True) + 1e-05)
    ).astype(jnp.bfloat16)


def gather_pieces(piece):
    ny = DP_SUB[0]
    own = piece[None]
    across = lax.ppermute(own, "dp", DP_X_SWAP)
    pair = jnp.concatenate([own, across])
    pair_keys = [(0, 0, 0), (0, 1, 0)]
    fwd1 = lax.ppermute(pair, "dp", DP_Y_FWD)
    fwd2 = lax.ppermute(fwd1, "dp", DP_Y_FWD)
    bwd1 = lax.ppermute(pair, "dp", DP_Y_BWD)
    shift = lambda keys, dy: [((k[0] + dy) % ny, k[1], k[2]) for k in keys]
    chip = jnp.concatenate([pair, fwd1, fwd2, bwd1])
    chip_keys = pair_keys + shift(pair_keys, ny - 1) + shift(pair_keys, ny - 2) + shift(pair_keys, 1)
    other_core = lax.ppermute(chip, "dp", DP_C_SWAP)
    return [
        ([(0, 0, 0)], own),
        ([(0, 1, 0)], across),
        (shift(pair_keys, ny - 1), fwd1),
        (shift(pair_keys, ny - 2), fwd2),
        (shift(pair_keys, 1), bwd1),
        ([(k[0], k[1], 1) for k in chip_keys], other_core),
    ]


def per_device(loader_rows, row_counts, row_targets, gate_weight, up_weight, down_weight):
    dp_count = lax.axis_size("dp")
    tp_count = lax.axis_size("tensor")
    slot_rows = loader_rows[0, 0]
    slot_targets = row_targets[0, 0]
    live_count = row_counts[0, 0]
    slot_count = slot_rows.shape[0]
    feature_count = slot_rows.shape[1]
    per_peer = slot_count // dp_count
    shard_rows = ROWS_GRP // tp_count
    slot_index = jnp.arange(slot_count, dtype=jnp.int32)
    is_live = slot_index < live_count
    peer_index = slot_targets // shard_rows
    row_place = slot_targets % shard_rows
    peer_hot = (
        (peer_index[:, None] == jnp.arange(dp_count, dtype=jnp.int32)[None, :]) & is_live[:, None]
    ).astype(jnp.int32)
    earlier = jnp.cumsum(peer_hot, axis=0) - peer_hot
    slot_rank = jnp.sum(earlier * peer_hot, axis=1)
    send_slot = peer_index * per_peer + slot_rank
    pick_matrix = (send_slot[None, :] == slot_index[:, None]) & is_live[None, :]
    outgoing = jnp.dot(
        pick_matrix.astype(jnp.bfloat16), slot_rows, preferred_element_type=jnp.float32
    ).astype(jnp.bfloat16)
    out_place = jnp.sum(jnp.where(pick_matrix, row_place[None, :] + 1, 0), axis=1) - 1
    place_cols = jnp.broadcast_to(out_place.astype(jnp.bfloat16)[:, None], (slot_count, 128))
    arrived = lax.all_to_all(
        jnp.concatenate([outgoing, place_cols], axis=1).reshape(dp_count, per_peer, feature_count + 128),
        "dp",
        split_axis=0,
        concat_axis=0,
        tiled=True,
    ).reshape(slot_count, feature_count + 128)
    arrived_place = arrived[:, feature_count].astype(jnp.int32)
    land_matrix = (
        arrived_place[None, :] == jnp.arange(shard_rows, dtype=jnp.int32)[:, None]
    ).astype(jnp.bfloat16)
    local_batch = jnp.dot(
        land_matrix, arrived[:, :feature_count], preferred_element_type=jnp.float32
    ).astype(jnp.bfloat16)

    ff_cols = gate_weight.shape[1]
    piece_rows = gate_weight.shape[0]
    buffers = gather_pieces(jnp.concatenate([gate_weight, up_weight], axis=1))
    keys = [k for ks, _ in buffers for k in ks]
    ny, nx, nc = DP_SUB
    me = lax.axis_index("dp")
    my_y, my_x, my_c = me // (nx * nc), (me // nc) % nx, me % nc
    piece_index = jnp.stack(
        [((my_y + k[0]) % ny) * nx * nc + ((my_x + k[1]) % nx) * nc + (my_c + k[2]) % nc for k in keys]
    ).astype(jnp.int32)

    nl, nz = TP_SUB
    travelling = normalize(local_batch)
    travelling = jnp.take(
        travelling.reshape(shard_rows, dp_count, piece_rows), piece_index, axis=1
    ).reshape(shard_rows, feature_count)
    on_core0 = (me % nc) == 0
    pick = lambda a, b: jnp.where(on_core0, a, b)
    ring_axes = ("dp", "tensor")
    my_pair = jnp.stack([travelling, lax.ppermute(travelling, "tensor", TP_L_SWAP)])
    other_pair = lax.ppermute(my_pair, "dp", DP_C_SWAP)
    carried = pick(jnp.stack([my_pair, other_pair]), jnp.stack([other_pair, my_pair]))
    arrivals = []
    for s in range(nz // 2):
        carried = lax.ppermute(carried, ring_axes, SPLIT_BOTH if s < nz // 2 - 1 else SPLIT_FWD_ONLY)
        arrivals.append(carried)
    mine = [pick(r[0], r[1]) for r in arrivals]
    theirs = jnp.stack([pick(r[1], r[0]) for r in arrivals])
    swapped = lax.ppermute(theirs, "dp", DP_C_SWAP)
    slots = [my_pair] + mine[: nz // 2 - 1] + [pick(mine[nz // 2 - 1], swapped[nz // 2 - 1])]
    slots = slots + [swapped[i] for i in range(nz // 2 - 1)]
    gathered = jnp.stack(slots)
    row_total = gathered.shape[0] * gathered.shape[1] * gathered.shape[2]
    normed = gathered.reshape(row_total, feature_count)

    act = None
    col = 0
    for ks, buf in buffers:
        width = len(ks) * piece_rows
        part = jnp.dot(
            normed[:, col : col + width],
            buf.reshape(width, 2 * ff_cols),
            preferred_element_type=jnp.float32,
        )
        act = part if act is None else act + part
        col += width
    gate_act = act[:, :ff_cols]
    up_act = act[:, ff_cols:]
    hidden = (jax.nn.silu(gate_act) * up_act).astype(jnp.bfloat16)
    term = jnp.dot(hidden, down_weight, preferred_element_type=jnp.float32).astype(jnp.bfloat16)
    blocks = term.reshape(nz, nl, shard_rows, feature_count)

    f32 = lambda v: v.astype(jnp.float32)
    half = nz // 2
    other = lax.ppermute(blocks[1 : half + 1], "dp", DP_C_SWAP)
    by_group = lambda own_part, other_part: pick(
        jnp.stack([own_part, other_part]), jnp.stack([other_part, own_part])
    )
    carried = by_group(pick(blocks[half], blocks[nz - 1]), pick(other[half - 1], other[half - 2]))
    for s in range(half):
        got = lax.ppermute(carried, ring_axes, SPLIT_BOTH if s < half - 1 else SPLIT_FWD_ONLY)
        if s < half - 2:
            add = by_group(pick(blocks[nz - 1 - s], blocks[nz - 2 - s]), pick(other[half - 2 - s], other[half - 3 - s]))
            carried = (f32(got) + f32(add)).astype(jnp.bfloat16)
        elif s == half - 2:
            core1_total = got
            add = by_group(blocks[nz - 1 - s], other[half - 2 - s])
            carried = (f32(got) + f32(add)).astype(jnp.bfloat16)
        else:
            chain_total = pick(got, core1_total)
    keep = pick(chain_total[0], chain_total[1])
    give = pick(chain_total[1], chain_total[0])
    from_other = lax.ppermute(give, "dp", DP_C_SWAP)
    column_sum = f32(keep) + f32(from_other) + f32(blocks[0])
    from_partner = lax.ppermute(column_sum[1].astype(jnp.bfloat16), "tensor", TP_L_SWAP)
    total = column_sum[0] + f32(from_partner)
    return (local_batch.astype(jnp.float32) + total).astype(jnp.bfloat16)


def solution(mesh):
    placed = (
        P("dp", "tensor", None, None),
        P("dp", "tensor"),
        P("dp", "tensor", None),
        P("dp", "tensor"),
        P("dp", "tensor"),
        P("tensor", None),
    )
    return jax.shard_map(
        per_device, mesh=mesh, in_specs=placed, out_specs=P(("dp", "tensor"), None), check_vma=False
    )
```

```python
import jax
import jax.numpy as jnp
from jax import lax
from jax.sharding import PartitionSpec as P

ROWS_GRP = 512
DP_SUB = (4, 2, 2)
TP_SUB = (2, 16)


def dp_perm(move):
    ny, nx, nc = DP_SUB
    pairs = []
    for y in range(ny):
        for x in range(nx):
            for c in range(nc):
                ty, tx, tc = move(y, x, c)
                pairs.append((y * nx * nc + x * nc + c, (ty % ny) * nx * nc + (tx % nx) * nc + tc % nc))
    return pairs


def tp_perm(move):
    nl, nz = TP_SUB
    pairs = []
    for l in range(nl):
        for z in range(nz):
            tl, tz = move(l, z)
            pairs.append((l * nz + z, (tl % nl) * nz + tz % nz))
    return pairs


DP_Y_FWD = dp_perm(lambda y, x, c: (y + 1, x, c))
DP_Y_BWD = dp_perm(lambda y, x, c: (y - 1, x, c))
DP_X_SWAP = dp_perm(lambda y, x, c: (y, x + 1, c))
DP_C_SWAP = dp_perm(lambda y, x, c: (y, x, c + 1))
TP_L_SWAP = tp_perm(lambda l, z: (l + 1, z))
TP_Z_FWD = tp_perm(lambda l, z: (l, z + 1))
TP_Z_BWD = tp_perm(lambda l, z: (l, z - 1))


RING_PIECES = 4


def ring_permute(x, perm):
    width = x.shape[-1] // RING_PIECES
    return jnp.concatenate(
        [lax.ppermute(x[..., i * width : (i + 1) * width], "tensor", perm) for i in range(RING_PIECES)], axis=-1
    )


def normalize(row_block):
    wide_rows = row_block.astype(jnp.float32)
    return (
        wide_rows * lax.rsqrt(jnp.mean(wide_rows * wide_rows, axis=1, keepdims=True) + 1e-05)
    ).astype(jnp.bfloat16)


def gather_pieces(piece):
    ny = DP_SUB[0]
    own = piece[None]
    across = lax.ppermute(own, "dp", DP_X_SWAP)
    pair = jnp.concatenate([own, across])
    pair_keys = [(0, 0, 0), (0, 1, 0)]
    fwd1 = lax.ppermute(pair, "dp", DP_Y_FWD)
    fwd2 = lax.ppermute(fwd1, "dp", DP_Y_FWD)
    bwd1 = lax.ppermute(pair, "dp", DP_Y_BWD)
    shift = lambda keys, dy: [((k[0] + dy) % ny, k[1], k[2]) for k in keys]
    chip = jnp.concatenate([pair, fwd1, fwd2, bwd1])
    chip_keys = pair_keys + shift(pair_keys, ny - 1) + shift(pair_keys, ny - 2) + shift(pair_keys, 1)
    other_core = lax.ppermute(chip, "dp", DP_C_SWAP)
    return [
        ([(0, 0, 0)], own),
        ([(0, 1, 0)], across),
        (shift(pair_keys, ny - 1), fwd1),
        (shift(pair_keys, ny - 2), fwd2),
        (shift(pair_keys, 1), bwd1),
        ([(k[0], k[1], 1) for k in chip_keys], other_core),
    ]


def per_device(loader_rows, row_counts, row_targets, gate_weight, up_weight, down_weight):
    dp_count = lax.axis_size("dp")
    tp_count = lax.axis_size("tensor")
    slot_rows = loader_rows[0, 0]
    slot_targets = row_targets[0, 0]
    live_count = row_counts[0, 0]
    slot_count = slot_rows.shape[0]
    feature_count = slot_rows.shape[1]
    per_peer = slot_count // dp_count
    shard_rows = ROWS_GRP // tp_count
    slot_index = jnp.arange(slot_count, dtype=jnp.int32)
    is_live = slot_index < live_count
    peer_index = slot_targets // shard_rows
    row_place = slot_targets % shard_rows
    peer_hot = (
        (peer_index[:, None] == jnp.arange(dp_count, dtype=jnp.int32)[None, :]) & is_live[:, None]
    ).astype(jnp.int32)
    earlier = jnp.cumsum(peer_hot, axis=0) - peer_hot
    slot_rank = jnp.sum(earlier * peer_hot, axis=1)
    send_slot = peer_index * per_peer + slot_rank
    pick_matrix = (send_slot[None, :] == slot_index[:, None]) & is_live[None, :]
    outgoing = jnp.dot(
        pick_matrix.astype(jnp.bfloat16), slot_rows, preferred_element_type=jnp.float32
    ).astype(jnp.bfloat16)
    out_place = jnp.sum(jnp.where(pick_matrix, row_place[None, :] + 1, 0), axis=1) - 1
    place_cols = jnp.broadcast_to(out_place.astype(jnp.bfloat16)[:, None], (slot_count, 128))
    arrived = lax.all_to_all(
        jnp.concatenate([outgoing, place_cols], axis=1).reshape(dp_count, per_peer, feature_count + 128),
        "dp",
        split_axis=0,
        concat_axis=0,
        tiled=True,
    ).reshape(slot_count, feature_count + 128)
    arrived_place = arrived[:, feature_count].astype(jnp.int32)
    land_matrix = (
        arrived_place[None, :] == jnp.arange(shard_rows, dtype=jnp.int32)[:, None]
    ).astype(jnp.bfloat16)
    local_batch = jnp.dot(
        land_matrix, arrived[:, :feature_count], preferred_element_type=jnp.float32
    ).astype(jnp.bfloat16)

    ff_cols = gate_weight.shape[1]
    piece_rows = gate_weight.shape[0]
    buffers = gather_pieces(jnp.concatenate([gate_weight, up_weight], axis=1))
    keys = [k for ks, _ in buffers for k in ks]
    ny, nx, nc = DP_SUB
    me = lax.axis_index("dp")
    my_y, my_x, my_c = me // (nx * nc), (me // nc) % nx, me % nc
    piece_index = jnp.stack(
        [((my_y + k[0]) % ny) * nx * nc + ((my_x + k[1]) % nx) * nc + (my_c + k[2]) % nc for k in keys]
    ).astype(jnp.int32)

    nl, nz = TP_SUB
    travelling = normalize(local_batch)
    travelling = jnp.take(
        travelling.reshape(shard_rows, dp_count, piece_rows), piece_index, axis=1
    ).reshape(shard_rows, feature_count)
    pair = jnp.stack([travelling, lax.ppermute(travelling, "tensor", TP_L_SWAP)])
    token_chunks = {0: pair}
    fwd = pair
    for s in range(nz // 2):
        fwd = ring_permute(fwd, TP_Z_FWD)
        token_chunks[nz - 1 - s] = fwd
    bwd = pair
    for s in range(nz // 2 - 1):
        bwd = ring_permute(bwd, TP_Z_BWD)
        token_chunks[s + 1] = bwd
    gathered = jnp.concatenate([token_chunks[k] for k in range(nz)], axis=0)
    row_total = gathered.shape[0] * gathered.shape[1]
    normed = gathered.reshape(row_total, feature_count)

    act = None
    col = 0
    for ks, buf in buffers:
        width = len(ks) * piece_rows
        part = jnp.dot(
            normed[:, col : col + width],
            buf.reshape(width, 2 * ff_cols),
            preferred_element_type=jnp.float32,
        )
        act = part if act is None else act + part
        col += width
    gate_act = act[:, :ff_cols]
    up_act = act[:, ff_cols:]
    hidden = (jax.nn.silu(gate_act) * up_act).astype(jnp.bfloat16)
    term = jnp.dot(hidden, down_weight, preferred_element_type=jnp.float32).astype(jnp.bfloat16)
    blocks = term.reshape(nz, nl, shard_rows, feature_count)

    fwd = blocks[nz // 2]
    for s in range(nz // 2):
        got = ring_permute(fwd, TP_Z_FWD)
        if s < nz // 2 - 1:
            fwd = (got.astype(jnp.float32) + blocks[nz // 2 - 1 - s].astype(jnp.float32)).astype(jnp.bfloat16)
        else:
            fwd_total = got
    bwd = blocks[nz // 2 + 1]
    for s in range(nz // 2 - 1):
        got = ring_permute(bwd, TP_Z_BWD)
        if s < nz // 2 - 2:
            bwd = (got.astype(jnp.float32) + blocks[nz // 2 + 2 + s].astype(jnp.float32)).astype(jnp.bfloat16)
        else:
            bwd_total = got
    column_sum = (
        fwd_total.astype(jnp.float32) + bwd_total.astype(jnp.float32) + blocks[0].astype(jnp.float32)
    )
    from_partner = lax.ppermute(column_sum[1].astype(jnp.bfloat16), "tensor", TP_L_SWAP)
    total = column_sum[0] + from_partner.astype(jnp.float32)
    return (local_batch.astype(jnp.float32) + total).astype(jnp.bfloat16)


def solution(mesh):
    placed = (
        P("dp", "tensor", None, None),
        P("dp", "tensor"),
        P("dp", "tensor", None),
        P("dp", "tensor"),
        P("dp", "tensor"),
        P("tensor", None),
    )
    return jax.shard_map(
        per_device, mesh=mesh, in_specs=placed, out_specs=P(("dp", "tensor"), None), check_vma=False
    )
```

```python
import jax
import jax.numpy as jnp
from jax import lax
from jax.sharding import PartitionSpec as P

ROWS_GRP = 512
DP_SUB = (4, 2, 2)
TP_SUB = (2, 16)


def dp_perm(move):
    ny, nx, nc = DP_SUB
    pairs = []
    for y in range(ny):
        for x in range(nx):
            for c in range(nc):
                ty, tx, tc = move(y, x, c)
                pairs.append((y * nx * nc + x * nc + c, (ty % ny) * nx * nc + (tx % nx) * nc + tc % nc))
    return pairs


def tp_perm(move):
    nl, nz = TP_SUB
    pairs = []
    for l in range(nl):
        for z in range(nz):
            tl, tz = move(l, z)
            pairs.append((l * nz + z, (tl % nl) * nz + tz % nz))
    return pairs


DP_Y_FWD = dp_perm(lambda y, x, c: (y + 1, x, c))
DP_Y_BWD = dp_perm(lambda y, x, c: (y - 1, x, c))
DP_X_SWAP = dp_perm(lambda y, x, c: (y, x + 1, c))
DP_C_SWAP = dp_perm(lambda y, x, c: (y, x, c + 1))
TP_L_SWAP = tp_perm(lambda l, z: (l + 1, z))
TP_Z_FWD = tp_perm(lambda l, z: (l, z + 1))
TP_Z_BWD = tp_perm(lambda l, z: (l, z - 1))


def normalize(row_block):
    wide_rows = row_block.astype(jnp.float32)
    return (
        wide_rows * lax.rsqrt(jnp.mean(wide_rows * wide_rows, axis=1, keepdims=True) + 1e-05)
    ).astype(jnp.bfloat16)


def gather_pieces(piece):
    ny = DP_SUB[0]
    own = piece[None]
    fwd1 = lax.ppermute(own, "dp", DP_Y_FWD)
    fwd2 = lax.ppermute(fwd1, "dp", DP_Y_FWD)
    bwd1 = lax.ppermute(own, "dp", DP_Y_BWD)
    col_keys = [(0, 0, 0), (ny - 1, 0, 0), (ny - 2, 0, 0), (1, 0, 0)]
    across = lax.ppermute(jnp.concatenate([own, fwd1, fwd2, bwd1]), "dp", DP_X_SWAP)
    across_keys = [(k[0], 1, 0) for k in col_keys]
    chip = jnp.concatenate([own, fwd1, fwd2, bwd1, across])
    other_core = lax.ppermute(chip, "dp", DP_C_SWAP)
    return [
        (col_keys[0:1], own),
        (col_keys[1:2], fwd1),
        (col_keys[2:3], fwd2),
        (col_keys[3:4], bwd1),
        (across_keys, across),
        ([(k[0], k[1], 1) for k in col_keys + across_keys], other_core),
    ]


def per_device(loader_rows, row_counts, row_targets, gate_weight, up_weight, down_weight):
    dp_count = lax.axis_size("dp")
    tp_count = lax.axis_size("tensor")
    slot_rows = loader_rows[0, 0]
    slot_targets = row_targets[0, 0]
    live_count = row_counts[0, 0]
    slot_count = slot_rows.shape[0]
    feature_count = slot_rows.shape[1]
    per_peer = slot_count // dp_count
    shard_rows = ROWS_GRP // tp_count
    slot_index = jnp.arange(slot_count, dtype=jnp.int32)
    is_live = slot_index < live_count
    peer_index = slot_targets // shard_rows
    row_place = slot_targets % shard_rows
    peer_hot = (
        (peer_index[:, None] == jnp.arange(dp_count, dtype=jnp.int32)[None, :]) & is_live[:, None]
    ).astype(jnp.int32)
    earlier = jnp.cumsum(peer_hot, axis=0) - peer_hot
    slot_rank = jnp.sum(earlier * peer_hot, axis=1)
    send_slot = peer_index * per_peer + slot_rank
    pick_matrix = (send_slot[None, :] == slot_index[:, None]) & is_live[None, :]
    outgoing = jnp.dot(
        pick_matrix.astype(jnp.bfloat16), slot_rows, preferred_element_type=jnp.float32
    ).astype(jnp.bfloat16)
    out_place = jnp.sum(jnp.where(pick_matrix, row_place[None, :] + 1, 0), axis=1) - 1
    place_cols = jnp.broadcast_to(out_place.astype(jnp.bfloat16)[:, None], (slot_count, 128))
    arrived = lax.all_to_all(
        jnp.concatenate([outgoing, place_cols], axis=1).reshape(dp_count, per_peer, feature_count + 128),
        "dp",
        split_axis=0,
        concat_axis=0,
        tiled=True,
    ).reshape(slot_count, feature_count + 128)
    arrived_place = arrived[:, feature_count].astype(jnp.int32)
    land_matrix = (
        arrived_place[None, :] == jnp.arange(shard_rows, dtype=jnp.int32)[:, None]
    ).astype(jnp.bfloat16)
    local_batch = jnp.dot(
        land_matrix, arrived[:, :feature_count], preferred_element_type=jnp.float32
    ).astype(jnp.bfloat16)

    ff_cols = gate_weight.shape[1]
    piece_rows = gate_weight.shape[0]
    buffers = gather_pieces(jnp.concatenate([gate_weight, up_weight], axis=1))
    keys = [k for ks, _ in buffers for k in ks]
    ny, nx, nc = DP_SUB
    me = lax.axis_index("dp")
    my_y, my_x, my_c = me // (nx * nc), (me // nc) % nx, me % nc
    piece_index = jnp.stack(
        [((my_y + k[0]) % ny) * nx * nc + ((my_x + k[1]) % nx) * nc + (my_c + k[2]) % nc for k in keys]
    ).astype(jnp.int32)

    nl, nz = TP_SUB
    travelling = normalize(local_batch)
    travelling = jnp.take(
        travelling.reshape(shard_rows, dp_count, piece_rows), piece_index, axis=1
    ).reshape(shard_rows, feature_count)
    pair = jnp.stack([travelling, lax.ppermute(travelling, "tensor", TP_L_SWAP)])
    token_chunks = {0: pair}
    fwd = pair
    for s in range(nz // 2):
        fwd = lax.ppermute(fwd, "tensor", TP_Z_FWD)
        token_chunks[nz - 1 - s] = fwd
    bwd = pair
    for s in range(nz // 2 - 1):
        bwd = lax.ppermute(bwd, "tensor", TP_Z_BWD)
        token_chunks[s + 1] = bwd
    gathered = jnp.concatenate([token_chunks[k] for k in range(nz)], axis=0)
    row_total = gathered.shape[0] * gathered.shape[1]
    normed = gathered.reshape(row_total, feature_count)

    act = None
    col = 0
    for ks, buf in buffers:
        width = len(ks) * piece_rows
        part = jnp.dot(
            normed[:, col : col + width],
            buf.reshape(width, 2 * ff_cols),
            preferred_element_type=jnp.float32,
        )
        act = part if act is None else act + part
        col += width
    gate_act = act[:, :ff_cols]
    up_act = act[:, ff_cols:]
    hidden = (jax.nn.silu(gate_act) * up_act).astype(jnp.bfloat16)
    term = jnp.dot(hidden, down_weight, preferred_element_type=jnp.float32).astype(jnp.bfloat16)
    blocks = term.reshape(nz, nl, shard_rows, feature_count)

    fwd = blocks[nz // 2]
    for s in range(nz // 2):
        got = lax.ppermute(fwd, "tensor", TP_Z_FWD)
        if s < nz // 2 - 1:
            fwd = (got.astype(jnp.float32) + blocks[nz // 2 - 1 - s].astype(jnp.float32)).astype(jnp.bfloat16)
        else:
            fwd_total = got
    bwd = blocks[nz // 2 + 1]
    for s in range(nz // 2 - 1):
        got = lax.ppermute(bwd, "tensor", TP_Z_BWD)
        if s < nz // 2 - 2:
            bwd = (got.astype(jnp.float32) + blocks[nz // 2 + 2 + s].astype(jnp.float32)).astype(jnp.bfloat16)
        else:
            bwd_total = got
    column_sum = (
        fwd_total.astype(jnp.float32) + bwd_total.astype(jnp.float32) + blocks[0].astype(jnp.float32)
    )
    from_partner = lax.ppermute(column_sum[1].astype(jnp.bfloat16), "tensor", TP_L_SWAP)
    total = column_sum[0] + from_partner.astype(jnp.float32)
    return (local_batch.astype(jnp.float32) + total).astype(jnp.bfloat16)


def solution(mesh):
    placed = (
        P("dp", "tensor", None, None),
        P("dp", "tensor"),
        P("dp", "tensor", None),
        P("dp", "tensor"),
        P("dp", "tensor"),
        P("tensor", None),
    )
    return jax.shard_map(
        per_device, mesh=mesh, in_specs=placed, out_specs=P(("dp", "tensor"), None), check_vma=False
    )
```

```python
import jax
import jax.numpy as jnp
from jax import lax
from jax.sharding import PartitionSpec as P

ROWS_GRP = 512
DP_SUB = (4, 2, 2)
TP_SUB = (2, 16)


def dp_perm(move):
    ny, nx, nc = DP_SUB
    pairs = []
    for y in range(ny):
        for x in range(nx):
            for c in range(nc):
                ty, tx, tc = move(y, x, c)
                pairs.append((y * nx * nc + x * nc + c, (ty % ny) * nx * nc + (tx % nx) * nc + tc % nc))
    return pairs


def tp_perm(move):
    nl, nz = TP_SUB
    pairs = []
    for l in range(nl):
        for z in range(nz):
            tl, tz = move(l, z)
            pairs.append((l * nz + z, (tl % nl) * nz + tz % nz))
    return pairs


DP_Y_FWD = dp_perm(lambda y, x, c: (y + 1, x, c))
DP_Y_BWD = dp_perm(lambda y, x, c: (y - 1, x, c))
DP_X_SWAP = dp_perm(lambda y, x, c: (y, x + 1, c))
DP_C_SWAP = dp_perm(lambda y, x, c: (y, x, c + 1))
TP_L_SWAP = tp_perm(lambda l, z: (l + 1, z))
TP_Z_FWD = tp_perm(lambda l, z: (l, z + 1))
TP_Z_BWD = tp_perm(lambda l, z: (l, z - 1))


def normalize(row_block):
    wide_rows = row_block.astype(jnp.float32)
    return (
        wide_rows * lax.rsqrt(jnp.mean(wide_rows * wide_rows, axis=1, keepdims=True) + 1e-05)
    ).astype(jnp.bfloat16)


def gather_pieces(piece):
    ny = DP_SUB[0]
    own = piece[None]
    fwd1 = lax.ppermute(own, "dp", DP_Y_FWD)
    fwd2 = lax.ppermute(fwd1, "dp", DP_Y_FWD)
    bwd1 = lax.ppermute(own, "dp", DP_Y_BWD)
    col_keys = [(0, 0, 0), (ny - 1, 0, 0), (ny - 2, 0, 0), (1, 0, 0)]
    across = lax.ppermute(jnp.concatenate([own, fwd1, fwd2, bwd1]), "dp", DP_X_SWAP)
    across_keys = [(k[0], 1, 0) for k in col_keys]
    chip = jnp.concatenate([own, fwd1, fwd2, bwd1, across])
    other_core = lax.ppermute(chip, "dp", DP_C_SWAP)
    return [
        (col_keys[0:1], own),
        (col_keys[1:2], fwd1),
        (col_keys[2:3], fwd2),
        (col_keys[3:4], bwd1),
        (across_keys, across),
        ([(k[0], k[1], 1) for k in col_keys + across_keys], other_core),
    ]


def per_device(loader_rows, row_counts, row_targets, gate_weight, up_weight, down_weight):
    dp_count = lax.axis_size("dp")
    tp_count = lax.axis_size("tensor")
    slot_rows = loader_rows[0, 0]
    slot_targets = row_targets[0, 0]
    live_count = row_counts[0, 0]
    slot_count = slot_rows.shape[0]
    feature_count = slot_rows.shape[1]
    per_peer = slot_count // dp_count
    shard_rows = ROWS_GRP // tp_count
    slot_index = jnp.arange(slot_count, dtype=jnp.int32)
    is_live = slot_index < live_count
    peer_index = slot_targets // shard_rows
    row_place = slot_targets % shard_rows
    peer_hot = (
        (peer_index[:, None] == jnp.arange(dp_count, dtype=jnp.int32)[None, :]) & is_live[:, None]
    ).astype(jnp.int32)
    earlier = jnp.cumsum(peer_hot, axis=0) - peer_hot
    slot_rank = jnp.sum(earlier * peer_hot, axis=1)
    send_slot = peer_index * per_peer + slot_rank
    pick_matrix = (send_slot[None, :] == slot_index[:, None]) & is_live[None, :]
    outgoing = jnp.dot(
        pick_matrix.astype(jnp.bfloat16), slot_rows, preferred_element_type=jnp.float32
    ).astype(jnp.bfloat16)
    out_place = jnp.sum(jnp.where(pick_matrix, row_place[None, :] + 1, 0), axis=1) - 1
    place_cols = jnp.broadcast_to(out_place.astype(jnp.bfloat16)[:, None], (slot_count, 128))
    arrived = lax.all_to_all(
        jnp.concatenate([outgoing, place_cols], axis=1).reshape(dp_count, per_peer, feature_count + 128),
        "dp",
        split_axis=0,
        concat_axis=0,
        tiled=True,
    ).reshape(slot_count, feature_count + 128)
    arrived_place = arrived[:, feature_count].astype(jnp.int32)
    land_matrix = (
        arrived_place[None, :] == jnp.arange(shard_rows, dtype=jnp.int32)[:, None]
    ).astype(jnp.bfloat16)
    local_batch = jnp.dot(
        land_matrix, arrived[:, :feature_count], preferred_element_type=jnp.float32
    ).astype(jnp.bfloat16)

    ff_cols = gate_weight.shape[1]
    piece_rows = gate_weight.shape[0]
    buffers = gather_pieces(jnp.concatenate([gate_weight, up_weight], axis=1))
    keys = [k for ks, _ in buffers for k in ks]
    ny, nx, nc = DP_SUB
    me = lax.axis_index("dp")
    my_y, my_x, my_c = me // (nx * nc), (me // nc) % nx, me % nc
    piece_index = jnp.stack(
        [((my_y + k[0]) % ny) * nx * nc + ((my_x + k[1]) % nx) * nc + (my_c + k[2]) % nc for k in keys]
    ).astype(jnp.int32)

    nl, nz = TP_SUB
    travelling = normalize(local_batch)
    travelling = jnp.take(
        travelling.reshape(shard_rows, dp_count, piece_rows), piece_index, axis=1
    ).reshape(shard_rows, feature_count)
    pair = jnp.stack([travelling, lax.ppermute(travelling, "tensor", TP_L_SWAP)])
    token_chunks = {0: pair}
    fwd = pair
    for s in range(nz // 2):
        fwd = lax.ppermute(fwd, "tensor", TP_Z_FWD)
        token_chunks[nz - 1 - s] = fwd
    bwd = pair
    for s in range(nz // 2 - 1):
        bwd = lax.ppermute(bwd, "tensor", TP_Z_BWD)
        token_chunks[s + 1] = bwd
    gathered = jnp.concatenate([token_chunks[k] for k in range(nz)], axis=0)
    row_total = gathered.shape[0] * gathered.shape[1]
    normed = gathered.reshape(row_total, feature_count)

    def ffn(rows):
        act = None
        col = 0
        for ks, buf in buffers:
            width = len(ks) * piece_rows
            part = jnp.dot(
                rows[:, col : col + width],
                buf.reshape(width, 2 * ff_cols),
                preferred_element_type=jnp.float32,
            )
            act = part if act is None else act + part
            col += width
        hidden = (jax.nn.silu(act[:, :ff_cols]) * act[:, ff_cols:]).astype(jnp.bfloat16)
        return jnp.dot(hidden, down_weight, preferred_element_type=jnp.float32).astype(jnp.bfloat16)

    chunk = nl * shard_rows
    lead = slice((nz // 2) * chunk, (nz // 2 + 2) * chunk)
    term = jnp.concatenate(
        [ffn(normed[: lead.start]), ffn(normed[lead]), ffn(normed[lead.stop :])], axis=0
    )
    blocks = term.reshape(nz, nl, shard_rows, feature_count)

    fwd = blocks[nz // 2]
    for s in range(nz // 2):
        got = lax.ppermute(fwd, "tensor", TP_Z_FWD)
        if s < nz // 2 - 1:
            fwd = (got.astype(jnp.float32) + blocks[nz // 2 - 1 - s].astype(jnp.float32)).astype(jnp.bfloat16)
        else:
            fwd_total = got
    bwd = blocks[nz // 2 + 1]
    for s in range(nz // 2 - 1):
        got = lax.ppermute(bwd, "tensor", TP_Z_BWD)
        if s < nz // 2 - 2:
            bwd = (got.astype(jnp.float32) + blocks[nz // 2 + 2 + s].astype(jnp.float32)).astype(jnp.bfloat16)
        else:
            bwd_total = got
    column_sum = (
        fwd_total.astype(jnp.float32) + bwd_total.astype(jnp.float32) + blocks[0].astype(jnp.float32)
    )
    from_partner = lax.ppermute(column_sum[1].astype(jnp.bfloat16), "tensor", TP_L_SWAP)
    total = column_sum[0] + from_partner.astype(jnp.float32)
    return (local_batch.astype(jnp.float32) + total).astype(jnp.bfloat16)


def solution(mesh):
    placed = (
        P("dp", "tensor", None, None),
        P("dp", "tensor"),
        P("dp", "tensor", None),
        P("dp", "tensor"),
        P("dp", "tensor"),
        P("tensor", None),
    )
    return jax.shard_map(
        per_device, mesh=mesh, in_specs=placed, out_specs=P(("dp", "tensor"), None), check_vma=False
    )
```

```python
import jax
import jax.numpy as jnp
from jax import lax
from jax.sharding import PartitionSpec as P

ROWS_GRP = 512
DP_SUB = (4, 2, 2)
TP_SUB = (2, 16)


def dp_perm(move):
    ny, nx, nc = DP_SUB
    pairs = []
    for y in range(ny):
        for x in range(nx):
            for c in range(nc):
                ty, tx, tc = move(y, x, c)
                pairs.append((y * nx * nc + x * nc + c, (ty % ny) * nx * nc + (tx % nx) * nc + tc % nc))
    return pairs


def tp_perm(move):
    nl, nz = TP_SUB
    pairs = []
    for l in range(nl):
        for z in range(nz):
            tl, tz = move(l, z)
            pairs.append((l * nz + z, (tl % nl) * nz + tz % nz))
    return pairs


DP_Y_FWD = dp_perm(lambda y, x, c: (y + 1, x, c))
DP_Y_BWD = dp_perm(lambda y, x, c: (y - 1, x, c))
DP_X_SWAP = dp_perm(lambda y, x, c: (y, x + 1, c))
DP_C_SWAP = dp_perm(lambda y, x, c: (y, x, c + 1))
TP_L_SWAP = tp_perm(lambda l, z: (l + 1, z))
TP_Z_FWD = tp_perm(lambda l, z: (l, z + 1))
TP_Z_BWD = tp_perm(lambda l, z: (l, z - 1))


def normalize(row_block):
    wide_rows = row_block.astype(jnp.float32)
    return (
        wide_rows * lax.rsqrt(jnp.mean(wide_rows * wide_rows, axis=1, keepdims=True) + 1e-05)
    ).astype(jnp.bfloat16)


def gather_pieces(piece):
    ny = DP_SUB[0]
    own = piece[None]
    fwd1 = lax.ppermute(own, "dp", DP_Y_FWD)
    fwd2 = lax.ppermute(fwd1, "dp", DP_Y_FWD)
    bwd1 = lax.ppermute(own, "dp", DP_Y_BWD)
    col_keys = [(0, 0, 0), (ny - 1, 0, 0), (ny - 2, 0, 0), (1, 0, 0)]
    across = lax.ppermute(jnp.concatenate([own, fwd1, fwd2, bwd1]), "dp", DP_X_SWAP)
    across_keys = [(k[0], 1, 0) for k in col_keys]
    chip = jnp.concatenate([own, fwd1, fwd2, bwd1, across])
    other_core = lax.ppermute(chip, "dp", DP_C_SWAP)
    return [
        (col_keys[0:1], own),
        (col_keys[1:2], fwd1),
        (col_keys[2:3], fwd2),
        (col_keys[3:4], bwd1),
        (across_keys, across),
        ([(k[0], k[1], 1) for k in col_keys + across_keys], other_core),
    ]


def per_device(loader_rows, row_counts, row_targets, gate_weight, up_weight, down_weight):
    dp_count = lax.axis_size("dp")
    tp_count = lax.axis_size("tensor")
    slot_rows = loader_rows[0, 0]
    slot_targets = row_targets[0, 0]
    live_count = row_counts[0, 0]
    slot_count = slot_rows.shape[0]
    feature_count = slot_rows.shape[1]
    per_peer = slot_count // dp_count
    shard_rows = ROWS_GRP // tp_count
    slot_index = jnp.arange(slot_count, dtype=jnp.int32)
    is_live = slot_index < live_count
    peer_index = slot_targets // shard_rows
    row_place = slot_targets % shard_rows
    peer_hot = (
        (peer_index[:, None] == jnp.arange(dp_count, dtype=jnp.int32)[None, :]) & is_live[:, None]
    ).astype(jnp.int32)
    earlier = jnp.cumsum(peer_hot, axis=0) - peer_hot
    slot_rank = jnp.sum(earlier * peer_hot, axis=1)
    send_slot = peer_index * per_peer + slot_rank
    pick_matrix = (send_slot[None, :] == slot_index[:, None]) & is_live[None, :]
    outgoing = jnp.dot(
        pick_matrix.astype(jnp.bfloat16), slot_rows, preferred_element_type=jnp.float32
    ).astype(jnp.bfloat16)
    out_place = jnp.sum(jnp.where(pick_matrix, row_place[None, :] + 1, 0), axis=1) - 1
    place_cols = jnp.broadcast_to(out_place.astype(jnp.bfloat16)[:, None], (slot_count, 128))
    arrived = lax.all_to_all(
        jnp.concatenate([outgoing, place_cols], axis=1).reshape(dp_count, per_peer, feature_count + 128),
        "dp",
        split_axis=0,
        concat_axis=0,
        tiled=True,
    ).reshape(slot_count, feature_count + 128)
    arrived_place = arrived[:, feature_count].astype(jnp.int32)
    land_matrix = (
        arrived_place[None, :] == jnp.arange(shard_rows, dtype=jnp.int32)[:, None]
    ).astype(jnp.bfloat16)
    local_batch = jnp.dot(
        land_matrix, arrived[:, :feature_count], preferred_element_type=jnp.float32
    ).astype(jnp.bfloat16)

    ff_cols = gate_weight.shape[1]
    piece_rows = gate_weight.shape[0]
    buffers = gather_pieces(jnp.concatenate([gate_weight, up_weight], axis=1))
    keys = [k for ks, _ in buffers for k in ks]
    ny, nx, nc = DP_SUB
    me = lax.axis_index("dp")
    my_y, my_x, my_c = me // (nx * nc), (me // nc) % nx, me % nc
    piece_index = jnp.stack(
        [((my_y + k[0]) % ny) * nx * nc + ((my_x + k[1]) % nx) * nc + (my_c + k[2]) % nc for k in keys]
    ).astype(jnp.int32)

    nl, nz = TP_SUB
    travelling = normalize(local_batch)
    travelling = jnp.take(
        travelling.reshape(shard_rows, dp_count, piece_rows), piece_index, axis=1
    ).reshape(shard_rows, feature_count)
    pair = jnp.stack([travelling, lax.ppermute(travelling, "tensor", TP_L_SWAP)])
    token_chunks = {0: pair}
    fwd = pair
    for s in range(nz // 2):
        fwd = lax.ppermute(fwd, "tensor", TP_Z_FWD)
        token_chunks[nz - 1 - s] = fwd
    bwd = pair
    for s in range(nz // 2 - 1):
        bwd = lax.ppermute(bwd, "tensor", TP_Z_BWD)
        token_chunks[s + 1] = bwd
    gathered = jnp.concatenate([token_chunks[k] for k in range(nz)], axis=0)
    row_total = gathered.shape[0] * gathered.shape[1]
    normed = gathered.reshape(row_total, feature_count)

    def ffn(rows):
        act = None
        col = 0
        for ks, buf in buffers:
            width = len(ks) * piece_rows
            part = jnp.dot(
                rows[:, col : col + width],
                buf.reshape(width, 2 * ff_cols),
                preferred_element_type=jnp.float32,
            )
            act = part if act is None else act + part
            col += width
        hidden = (jax.nn.silu(act[:, :ff_cols]) * act[:, ff_cols:]).astype(jnp.bfloat16)
        return jnp.dot(hidden, down_weight, preferred_element_type=jnp.float32).astype(jnp.bfloat16)

    chunk = nl * shard_rows
    blocks = {}
    for group in ([8, 9], [5, 6, 7, 10, 11, 12], [0, 1, 2, 3, 4, 13, 14, 15]):
        rows = jnp.concatenate([normed[k * chunk : (k + 1) * chunk] for k in group], axis=0)
        out = ffn(rows).reshape(len(group), nl, shard_rows, feature_count)
        for i, k in enumerate(group):
            blocks[k] = out[i]

    fwd = blocks[nz // 2]
    for s in range(nz // 2):
        got = lax.ppermute(fwd, "tensor", TP_Z_FWD)
        if s < nz // 2 - 1:
            fwd = (got.astype(jnp.float32) + blocks[nz // 2 - 1 - s].astype(jnp.float32)).astype(jnp.bfloat16)
        else:
            fwd_total = got
    bwd = blocks[nz // 2 + 1]
    for s in range(nz // 2 - 1):
        got = lax.ppermute(bwd, "tensor", TP_Z_BWD)
        if s < nz // 2 - 2:
            bwd = (got.astype(jnp.float32) + blocks[nz // 2 + 2 + s].astype(jnp.float32)).astype(jnp.bfloat16)
        else:
            bwd_total = got
    column_sum = (
        fwd_total.astype(jnp.float32) + bwd_total.astype(jnp.float32) + blocks[0].astype(jnp.float32)
    )
    from_partner = lax.ppermute(column_sum[1].astype(jnp.bfloat16), "tensor", TP_L_SWAP)
    total = column_sum[0] + from_partner.astype(jnp.float32)
    return (local_batch.astype(jnp.float32) + total).astype(jnp.bfloat16)


def solution(mesh):
    placed = (
        P("dp", "tensor", None, None),
        P("dp", "tensor"),
        P("dp", "tensor", None),
        P("dp", "tensor"),
        P("dp", "tensor"),
        P("tensor", None),
    )
    return jax.shard_map(
        per_device, mesh=mesh, in_specs=placed, out_specs=P(("dp", "tensor"), None), check_vma=False
    )
```

```python
import jax
import jax.numpy as jnp
from jax import lax
from jax.sharding import PartitionSpec as P

ROWS_GRP = 512
DP_SUB = (4, 2, 2)
TP_SUB = (2, 16)


def dp_perm(move):
    ny, nx, nc = DP_SUB
    pairs = []
    for y in range(ny):
        for x in range(nx):
            for c in range(nc):
                ty, tx, tc = move(y, x, c)
                pairs.append((y * nx * nc + x * nc + c, (ty % ny) * nx * nc + (tx % nx) * nc + tc % nc))
    return pairs


def tp_perm(move):
    nl, nz = TP_SUB
    pairs = []
    for l in range(nl):
        for z in range(nz):
            tl, tz = move(l, z)
            pairs.append((l * nz + z, (tl % nl) * nz + tz % nz))
    return pairs


DP_Y_FWD = dp_perm(lambda y, x, c: (y + 1, x, c))
DP_Y_BWD = dp_perm(lambda y, x, c: (y - 1, x, c))
DP_X_SWAP = dp_perm(lambda y, x, c: (y, x + 1, c))
DP_C_SWAP = dp_perm(lambda y, x, c: (y, x, c + 1))
TP_L_SWAP = tp_perm(lambda l, z: (l + 1, z))
TP_Z_FWD = tp_perm(lambda l, z: (l, z + 1))
TP_Z_BWD = tp_perm(lambda l, z: (l, z - 1))


def normalize(row_block):
    wide_rows = row_block.astype(jnp.float32)
    return (
        wide_rows * lax.rsqrt(jnp.mean(wide_rows * wide_rows, axis=1, keepdims=True) + 1e-05)
    ).astype(jnp.bfloat16)


def gather_pieces(piece):
    ny = DP_SUB[0]
    own = piece[None]
    fwd1 = lax.ppermute(own, "dp", DP_Y_FWD)
    fwd2 = lax.ppermute(fwd1, "dp", DP_Y_FWD)
    bwd1 = lax.ppermute(own, "dp", DP_Y_BWD)
    col_keys = [(0, 0, 0), (ny - 1, 0, 0), (ny - 2, 0, 0), (1, 0, 0)]
    across = lax.ppermute(jnp.concatenate([own, fwd1, fwd2, bwd1]), "dp", DP_X_SWAP)
    across_keys = [(k[0], 1, 0) for k in col_keys]
    chip = jnp.concatenate([own, fwd1, fwd2, bwd1, across])
    other_core = lax.ppermute(chip, "dp", DP_C_SWAP)
    return [
        (col_keys[0:1], own),
        (col_keys[1:2], fwd1),
        (col_keys[2:3], fwd2),
        (col_keys[3:4], bwd1),
        (across_keys, across),
        ([(k[0], k[1], 1) for k in col_keys + across_keys], other_core),
    ]


def per_device(loader_rows, row_counts, row_targets, gate_weight, up_weight, down_weight):
    dp_count = lax.axis_size("dp")
    tp_count = lax.axis_size("tensor")
    slot_rows = loader_rows[0, 0]
    slot_targets = row_targets[0, 0]
    live_count = row_counts[0, 0]
    slot_count = slot_rows.shape[0]
    feature_count = slot_rows.shape[1]
    per_peer = slot_count // dp_count
    shard_rows = ROWS_GRP // tp_count
    slot_index = jnp.arange(slot_count, dtype=jnp.int32)
    is_live = slot_index < live_count
    peer_index = slot_targets // shard_rows
    row_place = slot_targets % shard_rows
    peer_hot = (
        (peer_index[:, None] == jnp.arange(dp_count, dtype=jnp.int32)[None, :]) & is_live[:, None]
    ).astype(jnp.int32)
    earlier = jnp.cumsum(peer_hot, axis=0) - peer_hot
    slot_rank = jnp.sum(earlier * peer_hot, axis=1)
    send_slot = peer_index * per_peer + slot_rank
    pick_matrix = (send_slot[None, :] == slot_index[:, None]) & is_live[None, :]
    outgoing = jnp.dot(
        pick_matrix.astype(jnp.bfloat16), slot_rows, preferred_element_type=jnp.float32
    ).astype(jnp.bfloat16)
    out_place = jnp.sum(jnp.where(pick_matrix, row_place[None, :] + 1, 0), axis=1) - 1
    place_cols = jnp.broadcast_to(out_place.astype(jnp.bfloat16)[:, None], (slot_count, 128))
    arrived = lax.all_to_all(
        jnp.concatenate([outgoing, place_cols], axis=1).reshape(dp_count, per_peer, feature_count + 128),
        "dp",
        split_axis=0,
        concat_axis=0,
        tiled=True,
    ).reshape(slot_count, feature_count + 128)
    arrived_place = arrived[:, feature_count].astype(jnp.int32)
    land_matrix = (
        arrived_place[None, :] == jnp.arange(shard_rows, dtype=jnp.int32)[:, None]
    ).astype(jnp.bfloat16)
    local_batch = jnp.dot(
        land_matrix, arrived[:, :feature_count], preferred_element_type=jnp.float32
    ).astype(jnp.bfloat16)

    ff_cols = gate_weight.shape[1]
    piece_rows = gate_weight.shape[0]
    buffers = gather_pieces(jnp.concatenate([gate_weight, up_weight], axis=1))
    keys = [k for ks, _ in buffers for k in ks]
    ny, nx, nc = DP_SUB
    me = lax.axis_index("dp")
    my_y, my_x, my_c = me // (nx * nc), (me // nc) % nx, me % nc
    piece_index = jnp.stack(
        [((my_y + k[0]) % ny) * nx * nc + ((my_x + k[1]) % nx) * nc + (my_c + k[2]) % nc for k in keys]
    ).astype(jnp.int32)

    nl, nz = TP_SUB
    travelling = normalize(local_batch)
    travelling = jnp.take(
        travelling.reshape(shard_rows, dp_count, piece_rows), piece_index, axis=1
    ).reshape(shard_rows, feature_count)
    pair = jnp.stack([travelling, lax.ppermute(travelling, "tensor", TP_L_SWAP)])
    token_chunks = {0: pair}
    fwd = pair
    for s in range(nz // 2):
        fwd = lax.ppermute(fwd, "tensor", TP_Z_FWD)
        token_chunks[nz - 1 - s] = fwd
    bwd = pair
    for s in range(nz // 2 - 1):
        bwd = lax.ppermute(bwd, "tensor", TP_Z_BWD)
        token_chunks[s + 1] = bwd
    gathered = jnp.concatenate([token_chunks[k] for k in range(nz)], axis=0)
    row_total = gathered.shape[0] * gathered.shape[1]
    normed = gathered.reshape(row_total, feature_count)

    def ffn(rows):
        act = None
        col = 0
        for ks, buf in buffers:
            width = len(ks) * piece_rows
            part = jnp.dot(
                rows[:, col : col + width],
                buf.reshape(width, 2 * ff_cols),
                preferred_element_type=jnp.float32,
            )
            act = part if act is None else act + part
            col += width
        return (jax.nn.silu(act[:, :ff_cols]) * act[:, ff_cols:]).astype(jnp.bfloat16)

    def project(hidden):
        return jnp.dot(hidden, down_weight, preferred_element_type=jnp.float32).astype(jnp.bfloat16)

    chunk = nl * shard_rows
    blocks = {}
    groups = ([8, 9], [5, 6, 7, 10, 11, 12], [0, 1, 2, 3, 4, 13, 14, 15])
    hiddens = [
        ffn(jnp.concatenate([normed[k * chunk : (k + 1) * chunk] for k in group], axis=0)) for group in groups
    ]

    def place(g, hidden):
        out = project(hidden).reshape(len(groups[g]), nl, shard_rows, feature_count)
        for i, k in enumerate(groups[g]):
            blocks[k] = out[i]

    place(0, hiddens[0])

    fwd = blocks[nz // 2]
    for s in range(nz // 2):
        got = lax.ppermute(fwd, "tensor", TP_Z_FWD)
        if s < len(groups) - 1:
            late, got = lax.optimization_barrier((hiddens[s + 1], got))
            place(s + 1, late)
        if s < nz // 2 - 1:
            fwd = (got.astype(jnp.float32) + blocks[nz // 2 - 1 - s].astype(jnp.float32)).astype(jnp.bfloat16)
        else:
            fwd_total = got
    bwd = blocks[nz // 2 + 1]
    for s in range(nz // 2 - 1):
        got = lax.ppermute(bwd, "tensor", TP_Z_BWD)
        if s < nz // 2 - 2:
            bwd = (got.astype(jnp.float32) + blocks[nz // 2 + 2 + s].astype(jnp.float32)).astype(jnp.bfloat16)
        else:
            bwd_total = got
    column_sum = (
        fwd_total.astype(jnp.float32) + bwd_total.astype(jnp.float32) + blocks[0].astype(jnp.float32)
    )
    from_partner = lax.ppermute(column_sum[1].astype(jnp.bfloat16), "tensor", TP_L_SWAP)
    total = column_sum[0] + from_partner.astype(jnp.float32)
    return (local_batch.astype(jnp.float32) + total).astype(jnp.bfloat16)


def solution(mesh):
    placed = (
        P("dp", "tensor", None, None),
        P("dp", "tensor"),
        P("dp", "tensor", None),
        P("dp", "tensor"),
        P("dp", "tensor"),
        P("tensor", None),
    )
    return jax.shard_map(
        per_device, mesh=mesh, in_specs=placed, out_specs=P(("dp", "tensor"), None), check_vma=False
    )
```

```python
import jax
import jax.numpy as jnp
from jax import lax
from jax.sharding import PartitionSpec as P

ROWS_GRP = 512
DP_SUB = (4, 2, 2)
TP_SUB = (2, 16)


def dp_perm(move):
    ny, nx, nc = DP_SUB
    pairs = []
    for y in range(ny):
        for x in range(nx):
            for c in range(nc):
                ty, tx, tc = move(y, x, c)
                pairs.append((y * nx * nc + x * nc + c, (ty % ny) * nx * nc + (tx % nx) * nc + tc % nc))
    return pairs


def tp_perm(move):
    nl, nz = TP_SUB
    pairs = []
    for l in range(nl):
        for z in range(nz):
            tl, tz = move(l, z)
            pairs.append((l * nz + z, (tl % nl) * nz + tz % nz))
    return pairs


DP_Y_FWD = dp_perm(lambda y, x, c: (y + 1, x, c))
DP_Y_BWD = dp_perm(lambda y, x, c: (y - 1, x, c))
DP_X_SWAP = dp_perm(lambda y, x, c: (y, x + 1, c))
DP_C_SWAP = dp_perm(lambda y, x, c: (y, x, c + 1))
TP_L_SWAP = tp_perm(lambda l, z: (l + 1, z))
TP_Z_FWD = tp_perm(lambda l, z: (l, z + 1))
TP_Z_BWD = tp_perm(lambda l, z: (l, z - 1))


def normalize(row_block):
    wide_rows = row_block.astype(jnp.float32)
    return (
        wide_rows * lax.rsqrt(jnp.mean(wide_rows * wide_rows, axis=1, keepdims=True) + 1e-05)
    ).astype(jnp.bfloat16)


def gather_pieces(piece):
    ny = DP_SUB[0]
    own = piece[None]
    fwd1 = lax.ppermute(own, "dp", DP_Y_FWD)
    fwd2 = lax.ppermute(fwd1, "dp", DP_Y_FWD)
    bwd1 = lax.ppermute(own, "dp", DP_Y_BWD)
    col_keys = [(0, 0, 0), (ny - 1, 0, 0), (ny - 2, 0, 0), (1, 0, 0)]
    across = lax.ppermute(jnp.concatenate([own, fwd1, fwd2, bwd1]), "dp", DP_X_SWAP)
    across_keys = [(k[0], 1, 0) for k in col_keys]
    chip = jnp.concatenate([own, fwd1, fwd2, bwd1, across])
    other_core = lax.ppermute(chip, "dp", DP_C_SWAP)
    return [
        (col_keys[0:1], own),
        (col_keys[1:2], fwd1),
        (col_keys[2:3], fwd2),
        (col_keys[3:4], bwd1),
        (across_keys, across),
        ([(k[0], k[1], 1) for k in col_keys + across_keys], other_core),
    ]


def per_device(loader_rows, row_counts, row_targets, gate_weight, up_weight, down_weight):
    dp_count = lax.axis_size("dp")
    tp_count = lax.axis_size("tensor")
    slot_rows = loader_rows[0, 0]
    slot_targets = row_targets[0, 0]
    live_count = row_counts[0, 0]
    slot_count = slot_rows.shape[0]
    feature_count = slot_rows.shape[1]
    per_peer = slot_count // dp_count
    shard_rows = ROWS_GRP // tp_count
    slot_index = jnp.arange(slot_count, dtype=jnp.int32)
    is_live = slot_index < live_count
    peer_index = slot_targets // shard_rows
    row_place = slot_targets % shard_rows
    peer_hot = (
        (peer_index[:, None] == jnp.arange(dp_count, dtype=jnp.int32)[None, :]) & is_live[:, None]
    ).astype(jnp.int32)
    earlier = jnp.cumsum(peer_hot, axis=0) - peer_hot
    slot_rank = jnp.sum(earlier * peer_hot, axis=1)
    send_slot = peer_index * per_peer + slot_rank
    pick_matrix = (send_slot[None, :] == slot_index[:, None]) & is_live[None, :]
    outgoing = jnp.dot(
        pick_matrix.astype(jnp.bfloat16), slot_rows, preferred_element_type=jnp.float32
    ).astype(jnp.bfloat16)
    out_place = jnp.sum(jnp.where(pick_matrix, row_place[None, :] + 1, 0), axis=1) - 1
    place_cols = jnp.broadcast_to(out_place.astype(jnp.bfloat16)[:, None], (slot_count, 128))
    arrived = lax.all_to_all(
        jnp.concatenate([outgoing, place_cols], axis=1).reshape(dp_count, per_peer, feature_count + 128),
        "dp",
        split_axis=0,
        concat_axis=0,
        tiled=True,
    ).reshape(slot_count, feature_count + 128)
    arrived_place = arrived[:, feature_count].astype(jnp.int32)
    land_matrix = (
        arrived_place[None, :] == jnp.arange(shard_rows, dtype=jnp.int32)[:, None]
    ).astype(jnp.bfloat16)
    local_batch = jnp.dot(
        land_matrix, arrived[:, :feature_count], preferred_element_type=jnp.float32
    ).astype(jnp.bfloat16)

    ff_cols = gate_weight.shape[1]
    piece_rows = gate_weight.shape[0]
    buffers = gather_pieces(jnp.concatenate([gate_weight, up_weight], axis=1))
    keys = [k for ks, _ in buffers for k in ks]
    ny, nx, nc = DP_SUB
    me = lax.axis_index("dp")
    my_y, my_x, my_c = me // (nx * nc), (me // nc) % nx, me % nc
    piece_index = jnp.stack(
        [((my_y + k[0]) % ny) * nx * nc + ((my_x + k[1]) % nx) * nc + (my_c + k[2]) % nc for k in keys]
    ).astype(jnp.int32)

    nl, nz = TP_SUB
    travelling = normalize(local_batch)
    travelling = jnp.take(
        travelling.reshape(shard_rows, dp_count, piece_rows), piece_index, axis=1
    ).reshape(shard_rows, feature_count)
    pair = jnp.stack([travelling, lax.ppermute(travelling, "tensor", TP_L_SWAP)])
    token_chunks = {0: pair}
    fwd = pair
    for s in range(nz // 2 - 1):
        fwd = lax.ppermute(fwd, "tensor", TP_Z_FWD)
        token_chunks[nz - 1 - s] = fwd
    bwd = pair
    for s in range(nz // 2 - 1):
        bwd = lax.ppermute(bwd, "tensor", TP_Z_BWD)
        token_chunks[s + 1] = bwd
    half = feature_count // 2
    token_chunks[nz // 2] = jnp.concatenate(
        [
            lax.ppermute(fwd[..., :half], "tensor", TP_Z_FWD),
            lax.ppermute(bwd[..., half:], "tensor", TP_Z_BWD),
        ],
        axis=-1,
    )
    gathered = jnp.concatenate([token_chunks[k] for k in range(nz)], axis=0)
    row_total = gathered.shape[0] * gathered.shape[1]
    normed = gathered.reshape(row_total, feature_count)

    def ffn(rows):
        act = None
        col = 0
        for ks, buf in buffers:
            width = len(ks) * piece_rows
            part = jnp.dot(
                rows[:, col : col + width],
                buf.reshape(width, 2 * ff_cols),
                preferred_element_type=jnp.float32,
            )
            act = part if act is None else act + part
            col += width
        return (jax.nn.silu(act[:, :ff_cols]) * act[:, ff_cols:]).astype(jnp.bfloat16)

    def project(hidden):
        return jnp.dot(hidden, down_weight, preferred_element_type=jnp.float32).astype(jnp.bfloat16)

    chunk = nl * shard_rows
    blocks = {}
    groups = ([8, 9], [5, 6, 7, 10, 11, 12], [0, 1, 2, 3, 4, 13, 14, 15])
    hiddens = [
        ffn(jnp.concatenate([normed[k * chunk : (k + 1) * chunk] for k in group], axis=0)) for group in groups
    ]

    def place(g, hidden):
        out = project(hidden).reshape(len(groups[g]), nl, shard_rows, feature_count)
        for i, k in enumerate(groups[g]):
            blocks[k] = out[i]

    place(0, hiddens[0])

    fwd = blocks[nz // 2]
    for s in range(nz // 2):
        got = lax.ppermute(fwd, "tensor", TP_Z_FWD)
        if s < len(groups) - 1:
            late, got = lax.optimization_barrier((hiddens[s + 1], got))
            place(s + 1, late)
        if s < nz // 2 - 1:
            fwd = (got.astype(jnp.float32) + blocks[nz // 2 - 1 - s].astype(jnp.float32)).astype(jnp.bfloat16)
        else:
            fwd_total = got
    bwd = blocks[nz // 2 + 1]
    for s in range(nz // 2 - 1):
        got = lax.ppermute(bwd, "tensor", TP_Z_BWD)
        if s < nz // 2 - 2:
            bwd = (got.astype(jnp.float32) + blocks[nz // 2 + 2 + s].astype(jnp.float32)).astype(jnp.bfloat16)
        else:
            bwd_total = got
    column_sum = (
        fwd_total.astype(jnp.float32) + bwd_total.astype(jnp.float32) + blocks[0].astype(jnp.float32)
    )
    from_partner = lax.ppermute(column_sum[1].astype(jnp.bfloat16), "tensor", TP_L_SWAP)
    total = column_sum[0] + from_partner.astype(jnp.float32)
    return (local_batch.astype(jnp.float32) + total).astype(jnp.bfloat16)


def solution(mesh):
    placed = (
        P("dp", "tensor", None, None),
        P("dp", "tensor"),
        P("dp", "tensor", None),
        P("dp", "tensor"),
        P("dp", "tensor"),
        P("tensor", None),
    )
    return jax.shard_map(
        per_device, mesh=mesh, in_specs=placed, out_specs=P(("dp", "tensor"), None), check_vma=False
    )
```

```python
import jax
import jax.numpy as jnp
from jax import lax
from jax.sharding import PartitionSpec as P

ROWS_GRP = 512
DP_SUB = (4, 2, 2)
TP_SUB = (2, 16)


def dp_perm(move):
    ny, nx, nc = DP_SUB
    pairs = []
    for y in range(ny):
        for x in range(nx):
            for c in range(nc):
                ty, tx, tc = move(y, x, c)
                pairs.append((y * nx * nc + x * nc + c, (ty % ny) * nx * nc + (tx % nx) * nc + tc % nc))
    return pairs


def tp_perm(move):
    nl, nz = TP_SUB
    pairs = []
    for l in range(nl):
        for z in range(nz):
            tl, tz = move(l, z)
            pairs.append((l * nz + z, (tl % nl) * nz + tz % nz))
    return pairs


DP_Y_FWD = dp_perm(lambda y, x, c: (y + 1, x, c))
DP_Y_BWD = dp_perm(lambda y, x, c: (y - 1, x, c))
DP_X_SWAP = dp_perm(lambda y, x, c: (y, x + 1, c))
DP_C_SWAP = dp_perm(lambda y, x, c: (y, x, c + 1))
TP_L_SWAP = tp_perm(lambda l, z: (l + 1, z))
TP_Z_FWD = tp_perm(lambda l, z: (l, z + 1))
TP_Z_BWD = tp_perm(lambda l, z: (l, z - 1))


def normalize(row_block):
    wide_rows = row_block.astype(jnp.float32)
    return (
        wide_rows * lax.rsqrt(jnp.mean(wide_rows * wide_rows, axis=1, keepdims=True) + 1e-05)
    ).astype(jnp.bfloat16)


def gather_pieces(piece):
    ny = DP_SUB[0]
    own = piece[None]
    fwd1 = lax.ppermute(own, "dp", DP_Y_FWD)
    fwd2 = lax.ppermute(fwd1, "dp", DP_Y_FWD)
    bwd1 = lax.ppermute(own, "dp", DP_Y_BWD)
    col_keys = [(0, 0, 0), (ny - 1, 0, 0), (ny - 2, 0, 0), (1, 0, 0)]
    across = lax.ppermute(jnp.concatenate([own, fwd1, fwd2, bwd1]), "dp", DP_X_SWAP)
    across_keys = [(k[0], 1, 0) for k in col_keys]
    chip = jnp.concatenate([own, fwd1, fwd2, bwd1, across])
    other_core = lax.ppermute(chip, "dp", DP_C_SWAP)
    return [
        (col_keys[0:1], own),
        (col_keys[1:2], fwd1),
        (col_keys[2:3], fwd2),
        (col_keys[3:4], bwd1),
        (across_keys, across),
        ([(k[0], k[1], 1) for k in col_keys + across_keys], other_core),
    ]


def per_device(loader_rows, row_counts, row_targets, gate_weight, up_weight, down_weight):
    dp_count = lax.axis_size("dp")
    tp_count = lax.axis_size("tensor")
    slot_rows = loader_rows[0, 0]
    slot_targets = row_targets[0, 0]
    live_count = row_counts[0, 0]
    slot_count = slot_rows.shape[0]
    feature_count = slot_rows.shape[1]
    per_peer = slot_count // dp_count
    shard_rows = ROWS_GRP // tp_count
    slot_index = jnp.arange(slot_count, dtype=jnp.int32)
    is_live = slot_index < live_count
    peer_index = slot_targets // shard_rows
    row_place = slot_targets % shard_rows
    peer_hot = (
        (peer_index[:, None] == jnp.arange(dp_count, dtype=jnp.int32)[None, :]) & is_live[:, None]
    ).astype(jnp.int32)
    earlier = jnp.cumsum(peer_hot, axis=0) - peer_hot
    slot_rank = jnp.sum(earlier * peer_hot, axis=1)
    send_slot = peer_index * per_peer + slot_rank
    pick_matrix = (send_slot[None, :] == slot_index[:, None]) & is_live[None, :]
    outgoing = jnp.dot(
        pick_matrix.astype(jnp.bfloat16), slot_rows, preferred_element_type=jnp.float32
    ).astype(jnp.bfloat16)
    out_place = jnp.sum(jnp.where(pick_matrix, row_place[None, :] + 1, 0), axis=1) - 1
    place_cols = jnp.broadcast_to(out_place.astype(jnp.bfloat16)[:, None], (slot_count, 128))
    arrived = lax.all_to_all(
        jnp.concatenate([outgoing, place_cols], axis=1).reshape(dp_count, per_peer, feature_count + 128),
        "dp",
        split_axis=0,
        concat_axis=0,
        tiled=True,
    ).reshape(slot_count, feature_count + 128)
    arrived_place = arrived[:, feature_count].astype(jnp.int32)
    land_matrix = (
        arrived_place[None, :] == jnp.arange(shard_rows, dtype=jnp.int32)[:, None]
    ).astype(jnp.bfloat16)
    local_batch = jnp.dot(
        land_matrix, arrived[:, :feature_count], preferred_element_type=jnp.float32
    ).astype(jnp.bfloat16)

    ff_cols = gate_weight.shape[1]
    piece_rows = gate_weight.shape[0]
    buffers = gather_pieces(jnp.concatenate([gate_weight, up_weight], axis=1))
    keys = [k for ks, _ in buffers for k in ks]
    ny, nx, nc = DP_SUB
    me = lax.axis_index("dp")
    my_y, my_x, my_c = me // (nx * nc), (me // nc) % nx, me % nc
    piece_index = jnp.stack(
        [((my_y + k[0]) % ny) * nx * nc + ((my_x + k[1]) % nx) * nc + (my_c + k[2]) % nc for k in keys]
    ).astype(jnp.int32)

    nl, nz = TP_SUB
    travelling = normalize(local_batch)
    travelling = jnp.take(
        travelling.reshape(shard_rows, dp_count, piece_rows), piece_index, axis=1
    ).reshape(shard_rows, feature_count)
    pair = jnp.stack([travelling, lax.ppermute(travelling, "tensor", TP_L_SWAP)])
    token_chunks = {0: pair}
    fwd = pair
    for s in range(nz // 2 - 1):
        fwd = lax.ppermute(fwd, "tensor", TP_Z_FWD)
        token_chunks[nz - 1 - s] = fwd
    bwd = pair
    for s in range(nz // 2 - 1):
        bwd = lax.ppermute(bwd, "tensor", TP_Z_BWD)
        token_chunks[s + 1] = bwd
    half = feature_count // 2
    token_chunks[nz // 2] = jnp.concatenate(
        [
            lax.ppermute(fwd[..., :half], "tensor", TP_Z_FWD),
            lax.ppermute(bwd[..., half:], "tensor", TP_Z_BWD),
        ],
        axis=-1,
    )
    gathered = jnp.concatenate([token_chunks[k] for k in range(nz)], axis=0)
    row_total = gathered.shape[0] * gathered.shape[1]
    normed = gathered.reshape(row_total, feature_count)

    def ffn(rows):
        act = None
        col = 0
        for ks, buf in buffers:
            width = len(ks) * piece_rows
            part = jnp.dot(
                rows[:, col : col + width],
                buf.reshape(width, 2 * ff_cols),
                preferred_element_type=jnp.float32,
            )
            act = part if act is None else act + part
            col += width
        return (jax.nn.silu(act[:, :ff_cols]) * act[:, ff_cols:]).astype(jnp.bfloat16)

    def project(hidden):
        return jnp.dot(hidden, down_weight, preferred_element_type=jnp.float32).astype(jnp.bfloat16)

    chunk = nl * shard_rows
    blocks = {}
    groups = ([8, 9], [5, 6, 7, 10, 11, 12], [0, 1, 2, 3, 4, 13, 14, 15])
    hiddens = [
        ffn(jnp.concatenate([normed[k * chunk : (k + 1) * chunk] for k in group], axis=0)) for group in groups
    ]

    def place(g, hidden):
        out = project(hidden).reshape(len(groups[g]), nl, shard_rows, feature_count)
        for i, k in enumerate(groups[g]):
            blocks[k] = out[i]

    place(0, hiddens[0])

    f32 = lambda v: v.astype(jnp.float32)
    bf16 = lambda v: v.astype(jnp.bfloat16)
    half = feature_count // 2
    far = nz // 2
    fwd = blocks[far][..., :half]
    for s in range(far):
        got = lax.ppermute(fwd, "tensor", TP_Z_FWD)
        if s < len(groups) - 1:
            late, got = lax.optimization_barrier((hiddens[s + 1], got))
            place(s + 1, late)
        k = far - 1 - s
        if s == 0:
            fwd = jnp.concatenate([bf16(f32(got) + f32(blocks[k][..., :half])), blocks[k][..., half:]], axis=-1)
        elif s < far - 1:
            fwd = bf16(f32(got) + f32(blocks[k]))
        else:
            fwd_total = got
    bwd = blocks[far][..., half:]
    for s in range(far):
        got = lax.ppermute(bwd, "tensor", TP_Z_BWD)
        k = far + 1 + s
        if s == 0:
            bwd = jnp.concatenate([blocks[k][..., :half], bf16(f32(got) + f32(blocks[k][..., half:]))], axis=-1)
        elif s < far - 1:
            bwd = bf16(f32(got) + f32(blocks[k]))
        else:
            bwd_total = got
    column_sum = (
        fwd_total.astype(jnp.float32) + bwd_total.astype(jnp.float32) + blocks[0].astype(jnp.float32)
    )
    from_partner = lax.ppermute(column_sum[1].astype(jnp.bfloat16), "tensor", TP_L_SWAP)
    total = column_sum[0] + from_partner.astype(jnp.float32)
    return (local_batch.astype(jnp.float32) + total).astype(jnp.bfloat16)


def solution(mesh):
    placed = (
        P("dp", "tensor", None, None),
        P("dp", "tensor"),
        P("dp", "tensor", None),
        P("dp", "tensor"),
        P("dp", "tensor"),
        P("tensor", None),
    )
    return jax.shard_map(
        per_device, mesh=mesh, in_specs=placed, out_specs=P(("dp", "tensor"), None), check_vma=False
    )
```

```python
import jax
import jax.numpy as jnp
from jax import lax
from jax.sharding import PartitionSpec as P

ROWS_GRP = 512
DP_SUB = (4, 2, 2)
TP_SUB = (2, 16)


def dp_perm(move):
    ny, nx, nc = DP_SUB
    pairs = []
    for y in range(ny):
        for x in range(nx):
            for c in range(nc):
                ty, tx, tc = move(y, x, c)
                pairs.append((y * nx * nc + x * nc + c, (ty % ny) * nx * nc + (tx % nx) * nc + tc % nc))
    return pairs


def tp_perm(move):
    nl, nz = TP_SUB
    pairs = []
    for l in range(nl):
        for z in range(nz):
            tl, tz = move(l, z)
            pairs.append((l * nz + z, (tl % nl) * nz + tz % nz))
    return pairs


DP_Y_FWD = dp_perm(lambda y, x, c: (y + 1, x, c))
DP_Y_BWD = dp_perm(lambda y, x, c: (y - 1, x, c))
DP_X_SWAP = dp_perm(lambda y, x, c: (y, x + 1, c))
DP_C_SWAP = dp_perm(lambda y, x, c: (y, x, c + 1))
TP_L_SWAP = tp_perm(lambda l, z: (l + 1, z))
TP_Z_FWD = tp_perm(lambda l, z: (l, z + 1))
TP_Z_BWD = tp_perm(lambda l, z: (l, z - 1))
TP_DIAG_FWD = tp_perm(lambda l, z: (l + 1, z + 1))


def normalize(row_block):
    wide_rows = row_block.astype(jnp.float32)
    return (
        wide_rows * lax.rsqrt(jnp.mean(wide_rows * wide_rows, axis=1, keepdims=True) + 1e-05)
    ).astype(jnp.bfloat16)


def gather_pieces(piece):
    ny = DP_SUB[0]
    own = piece[None]
    fwd1 = lax.ppermute(own, "dp", DP_Y_FWD)
    fwd2 = lax.ppermute(fwd1, "dp", DP_Y_FWD)
    bwd1 = lax.ppermute(own, "dp", DP_Y_BWD)
    col_keys = [(0, 0, 0), (ny - 1, 0, 0), (ny - 2, 0, 0), (1, 0, 0)]
    across = lax.ppermute(jnp.concatenate([own, fwd1, fwd2, bwd1]), "dp", DP_X_SWAP)
    across_keys = [(k[0], 1, 0) for k in col_keys]
    chip = jnp.concatenate([own, fwd1, fwd2, bwd1, across])
    other_core = lax.ppermute(chip, "dp", DP_C_SWAP)
    return [
        (col_keys[0:1], own),
        (col_keys[1:2], fwd1),
        (col_keys[2:3], fwd2),
        (col_keys[3:4], bwd1),
        (across_keys, across),
        ([(k[0], k[1], 1) for k in col_keys + across_keys], other_core),
    ]


def per_device(loader_rows, row_counts, row_targets, gate_weight, up_weight, down_weight):
    dp_count = lax.axis_size("dp")
    tp_count = lax.axis_size("tensor")
    slot_rows = loader_rows[0, 0]
    slot_targets = row_targets[0, 0]
    live_count = row_counts[0, 0]
    slot_count = slot_rows.shape[0]
    feature_count = slot_rows.shape[1]
    per_peer = slot_count // dp_count
    shard_rows = ROWS_GRP // tp_count
    slot_index = jnp.arange(slot_count, dtype=jnp.int32)
    is_live = slot_index < live_count
    peer_index = slot_targets // shard_rows
    row_place = slot_targets % shard_rows
    peer_hot = (
        (peer_index[:, None] == jnp.arange(dp_count, dtype=jnp.int32)[None, :]) & is_live[:, None]
    ).astype(jnp.int32)
    earlier = jnp.cumsum(peer_hot, axis=0) - peer_hot
    slot_rank = jnp.sum(earlier * peer_hot, axis=1)
    send_slot = peer_index * per_peer + slot_rank
    pick_matrix = (send_slot[None, :] == slot_index[:, None]) & is_live[None, :]
    outgoing = jnp.dot(
        pick_matrix.astype(jnp.bfloat16), slot_rows, preferred_element_type=jnp.float32
    ).astype(jnp.bfloat16)
    out_place = jnp.sum(jnp.where(pick_matrix, row_place[None, :] + 1, 0), axis=1) - 1
    place_cols = jnp.broadcast_to(out_place.astype(jnp.bfloat16)[:, None], (slot_count, 128))
    arrived = lax.all_to_all(
        jnp.concatenate([outgoing, place_cols], axis=1).reshape(dp_count, per_peer, feature_count + 128),
        "dp",
        split_axis=0,
        concat_axis=0,
        tiled=True,
    ).reshape(slot_count, feature_count + 128)
    arrived_place = arrived[:, feature_count].astype(jnp.int32)
    land_matrix = (
        arrived_place[None, :] == jnp.arange(shard_rows, dtype=jnp.int32)[:, None]
    ).astype(jnp.bfloat16)
    local_batch = jnp.dot(
        land_matrix, arrived[:, :feature_count], preferred_element_type=jnp.float32
    ).astype(jnp.bfloat16)

    ff_cols = gate_weight.shape[1]
    piece_rows = gate_weight.shape[0]
    buffers = gather_pieces(jnp.concatenate([gate_weight, up_weight], axis=1))
    keys = [k for ks, _ in buffers for k in ks]
    ny, nx, nc = DP_SUB
    me = lax.axis_index("dp")
    my_y, my_x, my_c = me // (nx * nc), (me // nc) % nx, me % nc
    piece_index = jnp.stack(
        [((my_y + k[0]) % ny) * nx * nc + ((my_x + k[1]) % nx) * nc + (my_c + k[2]) % nc for k in keys]
    ).astype(jnp.int32)

    nl, nz = TP_SUB
    travelling = normalize(local_batch)
    travelling = jnp.take(
        travelling.reshape(shard_rows, dp_count, piece_rows), piece_index, axis=1
    ).reshape(shard_rows, feature_count)
    pair = jnp.stack([travelling, lax.ppermute(travelling, "tensor", TP_L_SWAP)])
    token_chunks = {0: pair}
    fwd = pair
    for s in range(nz // 2 - 1):
        fwd = lax.ppermute(fwd, "tensor", TP_Z_FWD)
        token_chunks[nz - 1 - s] = fwd
    bwd = pair
    for s in range(nz // 2 - 1):
        bwd = lax.ppermute(bwd, "tensor", TP_Z_BWD)
        token_chunks[s + 1] = bwd
    half = feature_count // 2
    token_chunks[nz // 2] = jnp.concatenate(
        [
            lax.ppermute(fwd[..., :half], "tensor", TP_Z_FWD),
            lax.ppermute(bwd[..., half:], "tensor", TP_Z_BWD),
        ],
        axis=-1,
    )
    gathered = jnp.concatenate([token_chunks[k] for k in range(nz)], axis=0)
    row_total = gathered.shape[0] * gathered.shape[1]
    normed = gathered.reshape(row_total, feature_count)

    def ffn(rows):
        act = None
        col = 0
        for ks, buf in buffers:
            width = len(ks) * piece_rows
            part = jnp.dot(
                rows[:, col : col + width],
                buf.reshape(width, 2 * ff_cols),
                preferred_element_type=jnp.float32,
            )
            act = part if act is None else act + part
            col += width
        return (jax.nn.silu(act[:, :ff_cols]) * act[:, ff_cols:]).astype(jnp.bfloat16)

    def project(hidden):
        return jnp.dot(hidden, down_weight, preferred_element_type=jnp.float32).astype(jnp.bfloat16)

    chunk = nl * shard_rows
    blocks = {}
    groups = ([8, 9], [5, 6, 7, 10, 11, 12], [0, 1, 2, 3, 4, 13, 14, 15])
    hiddens = [
        ffn(jnp.concatenate([normed[k * chunk : (k + 1) * chunk] for k in group], axis=0)) for group in groups
    ]

    def place(g, hidden):
        out = project(hidden).reshape(len(groups[g]), nl, shard_rows, feature_count)
        for i, k in enumerate(groups[g]):
            blocks[k] = out[i]

    place(0, hiddens[0])

    fwd = blocks[nz // 2]
    for s in range(nz // 2):
        if s == nz // 2 - 1:
            fwd_own = lax.ppermute(fwd[0], "tensor", TP_Z_FWD)
            fwd_diag = lax.ppermute(fwd[1], "tensor", TP_DIAG_FWD)
            break
        got = lax.ppermute(fwd, "tensor", TP_Z_FWD)
        if s < len(groups) - 1:
            late, got = lax.optimization_barrier((hiddens[s + 1], got))
            place(s + 1, late)
        fwd = (got.astype(jnp.float32) + blocks[nz // 2 - 1 - s].astype(jnp.float32)).astype(jnp.bfloat16)
    bwd = blocks[nz // 2 + 1]
    for s in range(nz // 2 - 1):
        got = lax.ppermute(bwd, "tensor", TP_Z_BWD)
        if s < nz // 2 - 2:
            bwd = (got.astype(jnp.float32) + blocks[nz // 2 + 2 + s].astype(jnp.float32)).astype(jnp.bfloat16)
        else:
            bwd_total = got
    f32 = lambda v: v.astype(jnp.float32)
    to_partner = (f32(bwd_total[1]) + f32(blocks[0][1])).astype(jnp.bfloat16)
    from_partner = lax.ppermute(to_partner, "tensor", TP_L_SWAP)
    total = f32(fwd_own) + f32(fwd_diag) + f32(bwd_total[0]) + f32(blocks[0][0]) + f32(from_partner)
    return (local_batch.astype(jnp.float32) + total).astype(jnp.bfloat16)


def solution(mesh):
    placed = (
        P("dp", "tensor", None, None),
        P("dp", "tensor"),
        P("dp", "tensor", None),
        P("dp", "tensor"),
        P("dp", "tensor"),
        P("tensor", None),
    )
    return jax.shard_map(
        per_device, mesh=mesh, in_specs=placed, out_specs=P(("dp", "tensor"), None), check_vma=False
    )
```

```python
import jax
import jax.numpy as jnp
from jax import lax
from jax.sharding import PartitionSpec as P

ROWS_GRP = 512
DP_SUB = (4, 2, 2)
TP_SUB = (2, 16)


def dp_perm(move):
    ny, nx, nc = DP_SUB
    pairs = []
    for y in range(ny):
        for x in range(nx):
            for c in range(nc):
                ty, tx, tc = move(y, x, c)
                pairs.append((y * nx * nc + x * nc + c, (ty % ny) * nx * nc + (tx % nx) * nc + tc % nc))
    return pairs


def tp_perm(move):
    nl, nz = TP_SUB
    pairs = []
    for l in range(nl):
        for z in range(nz):
            tl, tz = move(l, z)
            pairs.append((l * nz + z, (tl % nl) * nz + tz % nz))
    return pairs


DP_Y_FWD = dp_perm(lambda y, x, c: (y + 1, x, c))
DP_Y_BWD = dp_perm(lambda y, x, c: (y - 1, x, c))
DP_X_SWAP = dp_perm(lambda y, x, c: (y, x + 1, c))
DP_C_SWAP = dp_perm(lambda y, x, c: (y, x, c + 1))
TP_L_SWAP = tp_perm(lambda l, z: (l + 1, z))
TP_Z_FWD = tp_perm(lambda l, z: (l, z + 1))
TP_Z_BWD = tp_perm(lambda l, z: (l, z - 1))
TP_DIAG_FWD = tp_perm(lambda l, z: (l + 1, z + 1))
TP_DIAG_BWD = tp_perm(lambda l, z: (l + 1, z - 1))


def normalize(row_block):
    wide_rows = row_block.astype(jnp.float32)
    return (
        wide_rows * lax.rsqrt(jnp.mean(wide_rows * wide_rows, axis=1, keepdims=True) + 1e-05)
    ).astype(jnp.bfloat16)


def gather_pieces(piece):
    ny = DP_SUB[0]
    own = piece[None]
    fwd1 = lax.ppermute(own, "dp", DP_Y_FWD)
    fwd2 = lax.ppermute(fwd1, "dp", DP_Y_FWD)
    bwd1 = lax.ppermute(own, "dp", DP_Y_BWD)
    col_keys = [(0, 0, 0), (ny - 1, 0, 0), (ny - 2, 0, 0), (1, 0, 0)]
    across = lax.ppermute(jnp.concatenate([own, fwd1, fwd2, bwd1]), "dp", DP_X_SWAP)
    across_keys = [(k[0], 1, 0) for k in col_keys]
    chip = jnp.concatenate([own, fwd1, fwd2, bwd1, across])
    other_core = lax.ppermute(chip, "dp", DP_C_SWAP)
    return [
        (col_keys[0:1], own),
        (col_keys[1:2], fwd1),
        (col_keys[2:3], fwd2),
        (col_keys[3:4], bwd1),
        (across_keys, across),
        ([(k[0], k[1], 1) for k in col_keys + across_keys], other_core),
    ]


def per_device(loader_rows, row_counts, row_targets, gate_weight, up_weight, down_weight):
    dp_count = lax.axis_size("dp")
    tp_count = lax.axis_size("tensor")
    slot_rows = loader_rows[0, 0]
    slot_targets = row_targets[0, 0]
    live_count = row_counts[0, 0]
    slot_count = slot_rows.shape[0]
    feature_count = slot_rows.shape[1]
    per_peer = slot_count // dp_count
    shard_rows = ROWS_GRP // tp_count
    slot_index = jnp.arange(slot_count, dtype=jnp.int32)
    is_live = slot_index < live_count
    peer_index = slot_targets // shard_rows
    row_place = slot_targets % shard_rows
    peer_hot = (
        (peer_index[:, None] == jnp.arange(dp_count, dtype=jnp.int32)[None, :]) & is_live[:, None]
    ).astype(jnp.int32)
    earlier = jnp.cumsum(peer_hot, axis=0) - peer_hot
    slot_rank = jnp.sum(earlier * peer_hot, axis=1)
    send_slot = peer_index * per_peer + slot_rank
    pick_matrix = (send_slot[None, :] == slot_index[:, None]) & is_live[None, :]
    outgoing = jnp.dot(
        pick_matrix.astype(jnp.bfloat16), slot_rows, preferred_element_type=jnp.float32
    ).astype(jnp.bfloat16)
    out_place = jnp.sum(jnp.where(pick_matrix, row_place[None, :] + 1, 0), axis=1) - 1
    place_cols = jnp.broadcast_to(out_place.astype(jnp.bfloat16)[:, None], (slot_count, 128))
    arrived = lax.all_to_all(
        jnp.concatenate([outgoing, place_cols], axis=1).reshape(dp_count, per_peer, feature_count + 128),
        "dp",
        split_axis=0,
        concat_axis=0,
        tiled=True,
    ).reshape(slot_count, feature_count + 128)
    arrived_place = arrived[:, feature_count].astype(jnp.int32)
    land_matrix = (
        arrived_place[None, :] == jnp.arange(shard_rows, dtype=jnp.int32)[:, None]
    ).astype(jnp.bfloat16)
    local_batch = jnp.dot(
        land_matrix, arrived[:, :feature_count], preferred_element_type=jnp.float32
    ).astype(jnp.bfloat16)

    ff_cols = gate_weight.shape[1]
    piece_rows = gate_weight.shape[0]
    buffers = gather_pieces(jnp.concatenate([gate_weight, up_weight], axis=1))
    keys = [k for ks, _ in buffers for k in ks]
    ny, nx, nc = DP_SUB
    me = lax.axis_index("dp")
    my_y, my_x, my_c = me // (nx * nc), (me // nc) % nx, me % nc
    piece_index = jnp.stack(
        [((my_y + k[0]) % ny) * nx * nc + ((my_x + k[1]) % nx) * nc + (my_c + k[2]) % nc for k in keys]
    ).astype(jnp.int32)

    nl, nz = TP_SUB
    travelling = normalize(local_batch)
    travelling = jnp.take(
        travelling.reshape(shard_rows, dp_count, piece_rows), piece_index, axis=1
    ).reshape(shard_rows, feature_count)
    token_chunks = {0: jnp.stack([travelling, lax.ppermute(travelling, "tensor", TP_L_SWAP)])}
    fwd = jnp.stack(
        [lax.ppermute(travelling, "tensor", TP_Z_FWD), lax.ppermute(travelling, "tensor", TP_DIAG_FWD)]
    )
    token_chunks[nz - 1] = fwd
    for s in range(1, nz // 2 - 1):
        fwd = lax.ppermute(fwd, "tensor", TP_Z_FWD)
        token_chunks[nz - 1 - s] = fwd
    bwd = jnp.stack(
        [lax.ppermute(travelling, "tensor", TP_Z_BWD), lax.ppermute(travelling, "tensor", TP_DIAG_BWD)]
    )
    token_chunks[1] = bwd
    for s in range(1, nz // 2 - 1):
        bwd = lax.ppermute(bwd, "tensor", TP_Z_BWD)
        token_chunks[s + 1] = bwd
    half = feature_count // 2
    token_chunks[nz // 2] = jnp.concatenate(
        [
            lax.ppermute(fwd[..., :half], "tensor", TP_Z_FWD),
            lax.ppermute(bwd[..., half:], "tensor", TP_Z_BWD),
        ],
        axis=-1,
    )
    gathered = jnp.concatenate([token_chunks[k] for k in range(nz)], axis=0)
    row_total = gathered.shape[0] * gathered.shape[1]
    normed = gathered.reshape(row_total, feature_count)

    def ffn(rows):
        act = None
        col = 0
        for ks, buf in buffers:
            width = len(ks) * piece_rows
            part = jnp.dot(
                rows[:, col : col + width],
                buf.reshape(width, 2 * ff_cols),
                preferred_element_type=jnp.float32,
            )
            act = part if act is None else act + part
            col += width
        return (jax.nn.silu(act[:, :ff_cols]) * act[:, ff_cols:]).astype(jnp.bfloat16)

    def project(hidden):
        return jnp.dot(hidden, down_weight, preferred_element_type=jnp.float32).astype(jnp.bfloat16)

    chunk = nl * shard_rows
    blocks = {}
    groups = ([8, 9], [5, 6, 7, 10, 11, 12], [0, 1, 2, 3, 4, 13, 14, 15])
    hiddens = [
        ffn(jnp.concatenate([normed[k * chunk : (k + 1) * chunk] for k in group], axis=0)) for group in groups
    ]

    def place(g, hidden):
        out = project(hidden).reshape(len(groups[g]), nl, shard_rows, feature_count)
        for i, k in enumerate(groups[g]):
            blocks[k] = out[i]

    place(0, hiddens[0])

    fwd = blocks[nz // 2]
    for s in range(nz // 2):
        if s == nz // 2 - 1:
            fwd_own = lax.ppermute(fwd[0], "tensor", TP_Z_FWD)
            fwd_diag = lax.ppermute(fwd[1], "tensor", TP_DIAG_FWD)
            break
        got = lax.ppermute(fwd, "tensor", TP_Z_FWD)
        if s < len(groups) - 1:
            late, got = lax.optimization_barrier((hiddens[s + 1], got))
            place(s + 1, late)
        fwd = (got.astype(jnp.float32) + blocks[nz // 2 - 1 - s].astype(jnp.float32)).astype(jnp.bfloat16)
    bwd = blocks[nz // 2 + 1]
    for s in range(nz // 2 - 1):
        got = lax.ppermute(bwd, "tensor", TP_Z_BWD)
        if s < nz // 2 - 2:
            bwd = (got.astype(jnp.float32) + blocks[nz // 2 + 2 + s].astype(jnp.float32)).astype(jnp.bfloat16)
        else:
            bwd_total = got
    f32 = lambda v: v.astype(jnp.float32)
    to_partner = (f32(bwd_total[1]) + f32(blocks[0][1])).astype(jnp.bfloat16)
    from_partner = lax.ppermute(to_partner, "tensor", TP_L_SWAP)
    total = f32(fwd_own) + f32(fwd_diag) + f32(bwd_total[0]) + f32(blocks[0][0]) + f32(from_partner)
    return (local_batch.astype(jnp.float32) + total).astype(jnp.bfloat16)


def solution(mesh):
    placed = (
        P("dp", "tensor", None, None),
        P("dp", "tensor"),
        P("dp", "tensor", None),
        P("dp", "tensor"),
        P("dp", "tensor"),
        P("tensor", None),
    )
    return jax.shard_map(
        per_device, mesh=mesh, in_specs=placed, out_specs=P(("dp", "tensor"), None), check_vma=False
    )
```

```python
import jax
import jax.numpy as jnp
from jax import lax
from jax.sharding import PartitionSpec as P

ROWS_GRP = 512
DP_SUB = (4, 2, 2)
TP_SUB = (2, 16)


def dp_perm(move):
    ny, nx, nc = DP_SUB
    pairs = []
    for y in range(ny):
        for x in range(nx):
            for c in range(nc):
                ty, tx, tc = move(y, x, c)
                pairs.append((y * nx * nc + x * nc + c, (ty % ny) * nx * nc + (tx % nx) * nc + tc % nc))
    return pairs


def tp_perm(move):
    nl, nz = TP_SUB
    pairs = []
    for l in range(nl):
        for z in range(nz):
            tl, tz = move(l, z)
            pairs.append((l * nz + z, (tl % nl) * nz + tz % nz))
    return pairs


DP_Y_FWD = dp_perm(lambda y, x, c: (y + 1, x, c))
DP_Y_BWD = dp_perm(lambda y, x, c: (y - 1, x, c))
DP_X_SWAP = dp_perm(lambda y, x, c: (y, x + 1, c))
DP_C_SWAP = dp_perm(lambda y, x, c: (y, x, c + 1))
TP_L_SWAP = tp_perm(lambda l, z: (l + 1, z))
TP_Z_FWD = tp_perm(lambda l, z: (l, z + 1))
TP_Z_BWD = tp_perm(lambda l, z: (l, z - 1))
TP_DIAG_FWD = tp_perm(lambda l, z: (l + 1, z + 1))


def normalize(row_block):
    wide_rows = row_block.astype(jnp.float32)
    return (
        wide_rows * lax.rsqrt(jnp.mean(wide_rows * wide_rows, axis=1, keepdims=True) + 1e-05)
    ).astype(jnp.bfloat16)


def gather_pieces(piece):
    ny = DP_SUB[0]
    own = piece[None]
    fwd1 = lax.ppermute(own, "dp", DP_Y_FWD)
    fwd2 = lax.ppermute(fwd1, "dp", DP_Y_FWD)
    bwd1 = lax.ppermute(own, "dp", DP_Y_BWD)
    col_keys = [(0, 0, 0), (ny - 1, 0, 0), (ny - 2, 0, 0), (1, 0, 0)]
    across = lax.ppermute(jnp.concatenate([own, fwd1, fwd2, bwd1]), "dp", DP_X_SWAP)
    across_keys = [(k[0], 1, 0) for k in col_keys]
    chip = jnp.concatenate([own, fwd1, fwd2, bwd1, across])
    other_core = lax.ppermute(chip, "dp", DP_C_SWAP)
    return [
        (col_keys[0:1], own),
        (col_keys[1:2], fwd1),
        (col_keys[2:3], fwd2),
        (col_keys[3:4], bwd1),
        (across_keys, across),
        ([(k[0], k[1], 1) for k in col_keys + across_keys], other_core),
    ]


def per_device(loader_rows, row_counts, row_targets, gate_weight, up_weight, down_weight):
    dp_count = lax.axis_size("dp")
    tp_count = lax.axis_size("tensor")
    slot_rows = loader_rows[0, 0]
    slot_targets = row_targets[0, 0]
    live_count = row_counts[0, 0]
    slot_count = slot_rows.shape[0]
    feature_count = slot_rows.shape[1]
    per_peer = slot_count // dp_count
    shard_rows = ROWS_GRP // tp_count
    slot_index = jnp.arange(slot_count, dtype=jnp.int32)
    is_live = slot_index < live_count
    peer_index = slot_targets // shard_rows
    row_place = slot_targets % shard_rows
    peer_hot = (
        (peer_index[:, None] == jnp.arange(dp_count, dtype=jnp.int32)[None, :]) & is_live[:, None]
    ).astype(jnp.int32)
    earlier = jnp.cumsum(peer_hot, axis=0) - peer_hot
    slot_rank = jnp.sum(earlier * peer_hot, axis=1)
    send_slot = peer_index * per_peer + slot_rank
    pick_matrix = (send_slot[None, :] == slot_index[:, None]) & is_live[None, :]
    outgoing = jnp.dot(
        pick_matrix.astype(jnp.bfloat16), slot_rows, preferred_element_type=jnp.float32
    ).astype(jnp.bfloat16)
    out_place = jnp.sum(jnp.where(pick_matrix, row_place[None, :] + 1, 0), axis=1) - 1
    place_cols = jnp.broadcast_to(out_place.astype(jnp.bfloat16)[:, None], (slot_count, 128))
    arrived = lax.all_to_all(
        jnp.concatenate([outgoing, place_cols], axis=1).reshape(dp_count, per_peer, feature_count + 128),
        "dp",
        split_axis=0,
        concat_axis=0,
        tiled=True,
    ).reshape(slot_count, feature_count + 128)
    arrived_place = arrived[:, feature_count].astype(jnp.int32)
    land_matrix = (
        arrived_place[None, :] == jnp.arange(shard_rows, dtype=jnp.int32)[:, None]
    ).astype(jnp.bfloat16)
    local_batch = jnp.dot(
        land_matrix, arrived[:, :feature_count], preferred_element_type=jnp.float32
    ).astype(jnp.bfloat16)

    ff_cols = gate_weight.shape[1]
    piece_rows = gate_weight.shape[0]
    buffers = gather_pieces(jnp.concatenate([gate_weight, up_weight], axis=1))
    keys = [k for ks, _ in buffers for k in ks]
    ny, nx, nc = DP_SUB
    me = lax.axis_index("dp")
    my_y, my_x, my_c = me // (nx * nc), (me // nc) % nx, me % nc
    piece_index = jnp.stack(
        [((my_y + k[0]) % ny) * nx * nc + ((my_x + k[1]) % nx) * nc + (my_c + k[2]) % nc for k in keys]
    ).astype(jnp.int32)

    nl, nz = TP_SUB
    travelling = normalize(local_batch)
    travelling = jnp.take(
        travelling.reshape(shard_rows, dp_count, piece_rows), piece_index, axis=1
    ).reshape(shard_rows, feature_count)
    pair = jnp.stack([travelling, lax.ppermute(travelling, "tensor", TP_L_SWAP)])
    token_chunks = {0: pair}
    fwd = pair
    for s in range(nz // 2 - 1):
        fwd = lax.ppermute(fwd, "tensor", TP_Z_FWD)
        token_chunks[nz - 1 - s] = fwd
    bwd = pair
    for s in range(nz // 2 - 1):
        bwd = lax.ppermute(bwd, "tensor", TP_Z_BWD)
        token_chunks[s + 1] = bwd
    half = feature_count // 2
    token_chunks[nz // 2] = jnp.concatenate(
        [
            lax.ppermute(fwd[..., :half], "tensor", TP_Z_FWD),
            lax.ppermute(bwd[..., half:], "tensor", TP_Z_BWD),
        ],
        axis=-1,
    )
    gathered = jnp.concatenate([token_chunks[k] for k in range(nz)], axis=0)
    row_total = gathered.shape[0] * gathered.shape[1]
    normed = gathered.reshape(row_total, feature_count)

    def ffn(rows):
        act = None
        col = 0
        for ks, buf in buffers:
            width = len(ks) * piece_rows
            part = jnp.dot(
                rows[:, col : col + width],
                buf.reshape(width, 2 * ff_cols),
                preferred_element_type=jnp.float32,
            )
            act = part if act is None else act + part
            col += width
        return (jax.nn.silu(act[:, :ff_cols]) * act[:, ff_cols:]).astype(jnp.bfloat16)

    def project(hidden):
        return jnp.dot(hidden, down_weight, preferred_element_type=jnp.float32).astype(jnp.bfloat16)

    chunk = nl * shard_rows
    blocks = {}
    groups = ([8, 9], [0, 1, 2, 3, 4, 5, 6, 7, 10, 11, 12, 13, 14, 15])
    hiddens = [
        ffn(jnp.concatenate([normed[k * chunk : (k + 1) * chunk] for k in group], axis=0)) for group in groups
    ]

    def place(g, hidden):
        out = project(hidden).reshape(len(groups[g]), nl, shard_rows, feature_count)
        for i, k in enumerate(groups[g]):
            blocks[k] = out[i]

    place(0, hiddens[0])

    fwd = blocks[nz // 2]
    for s in range(nz // 2):
        if s == nz // 2 - 1:
            fwd_own = lax.ppermute(fwd[0], "tensor", TP_Z_FWD)
            fwd_diag = lax.ppermute(fwd[1], "tensor", TP_DIAG_FWD)
            break
        got = lax.ppermute(fwd, "tensor", TP_Z_FWD)
        if s < len(groups) - 1:
            late, got = lax.optimization_barrier((hiddens[s + 1], got))
            place(s + 1, late)
        fwd = (got.astype(jnp.float32) + blocks[nz // 2 - 1 - s].astype(jnp.float32)).astype(jnp.bfloat16)
    bwd = blocks[nz // 2 + 1]
    for s in range(nz // 2 - 1):
        got = lax.ppermute(bwd, "tensor", TP_Z_BWD)
        if s < nz // 2 - 2:
            bwd = (got.astype(jnp.float32) + blocks[nz // 2 + 2 + s].astype(jnp.float32)).astype(jnp.bfloat16)
        else:
            bwd_total = got
    f32 = lambda v: v.astype(jnp.float32)
    to_partner = (f32(bwd_total[1]) + f32(blocks[0][1])).astype(jnp.bfloat16)
    from_partner = lax.ppermute(to_partner, "tensor", TP_L_SWAP)
    total = f32(fwd_own) + f32(fwd_diag) + f32(bwd_total[0]) + f32(blocks[0][0]) + f32(from_partner)
    return (local_batch.astype(jnp.float32) + total).astype(jnp.bfloat16)


def solution(mesh):
    placed = (
        P("dp", "tensor", None, None),
        P("dp", "tensor"),
        P("dp", "tensor", None),
        P("dp", "tensor"),
        P("dp", "tensor"),
        P("tensor", None),
    )
    return jax.shard_map(
        per_device, mesh=mesh, in_specs=placed, out_specs=P(("dp", "tensor"), None), check_vma=False
    )
```

```python
import jax
import jax.numpy as jnp
from jax import lax
from jax.sharding import PartitionSpec as P

ROWS_GRP = 512
DP_SUB = (4, 2, 2)
TP_SUB = (2, 16)


def dp_perm(move):
    ny, nx, nc = DP_SUB
    pairs = []
    for y in range(ny):
        for x in range(nx):
            for c in range(nc):
                ty, tx, tc = move(y, x, c)
                pairs.append((y * nx * nc + x * nc + c, (ty % ny) * nx * nc + (tx % nx) * nc + tc % nc))
    return pairs


def tp_perm(move):
    nl, nz = TP_SUB
    pairs = []
    for l in range(nl):
        for z in range(nz):
            tl, tz = move(l, z)
            pairs.append((l * nz + z, (tl % nl) * nz + tz % nz))
    return pairs


DP_Y_FWD = dp_perm(lambda y, x, c: (y + 1, x, c))
DP_Y_BWD = dp_perm(lambda y, x, c: (y - 1, x, c))
DP_X_SWAP = dp_perm(lambda y, x, c: (y, x + 1, c))
DP_C_SWAP = dp_perm(lambda y, x, c: (y, x, c + 1))
TP_L_SWAP = tp_perm(lambda l, z: (l + 1, z))
TP_Z_FWD = tp_perm(lambda l, z: (l, z + 1))
TP_Z_BWD = tp_perm(lambda l, z: (l, z - 1))
TP_DIAG_FWD = tp_perm(lambda l, z: (l + 1, z + 1))


def normalize(row_block):
    wide_rows = row_block.astype(jnp.float32)
    return (
        wide_rows * lax.rsqrt(jnp.mean(wide_rows * wide_rows, axis=1, keepdims=True) + 1e-05)
    ).astype(jnp.bfloat16)


def gather_pieces(piece):
    ny = DP_SUB[0]
    own = piece[None]
    fwd1 = lax.ppermute(own, "dp", DP_Y_FWD)
    fwd2 = lax.ppermute(fwd1, "dp", DP_Y_FWD)
    bwd1 = lax.ppermute(own, "dp", DP_Y_BWD)
    col_keys = [(0, 0, 0), (ny - 1, 0, 0), (ny - 2, 0, 0), (1, 0, 0)]
    across = lax.ppermute(jnp.concatenate([own, fwd1, fwd2, bwd1]), "dp", DP_X_SWAP)
    across_keys = [(k[0], 1, 0) for k in col_keys]
    chip = jnp.concatenate([own, fwd1, fwd2, bwd1, across])
    other_core = lax.ppermute(chip, "dp", DP_C_SWAP)
    return [
        (col_keys[0:1], own),
        (col_keys[1:2], fwd1),
        (col_keys[2:3], fwd2),
        (col_keys[3:4], bwd1),
        (across_keys, across),
        ([(k[0], k[1], 1) for k in col_keys + across_keys], other_core),
    ]


def per_device(loader_rows, row_counts, row_targets, gate_weight, up_weight, down_weight):
    dp_count = lax.axis_size("dp")
    tp_count = lax.axis_size("tensor")
    slot_rows = loader_rows[0, 0]
    slot_targets = row_targets[0, 0]
    live_count = row_counts[0, 0]
    slot_count = slot_rows.shape[0]
    feature_count = slot_rows.shape[1]
    per_peer = slot_count // dp_count
    shard_rows = ROWS_GRP // tp_count
    slot_index = jnp.arange(slot_count, dtype=jnp.int32)
    is_live = slot_index < live_count
    peer_index = slot_targets // shard_rows
    row_place = slot_targets % shard_rows
    peer_hot = (
        (peer_index[:, None] == jnp.arange(dp_count, dtype=jnp.int32)[None, :]) & is_live[:, None]
    ).astype(jnp.int32)
    earlier = jnp.cumsum(peer_hot, axis=0) - peer_hot
    slot_rank = jnp.sum(earlier * peer_hot, axis=1)
    send_slot = peer_index * per_peer + slot_rank
    pick_matrix = (send_slot[None, :] == slot_index[:, None]) & is_live[None, :]
    outgoing = jnp.dot(
        pick_matrix.astype(jnp.bfloat16), slot_rows, preferred_element_type=jnp.float32
    ).astype(jnp.bfloat16)
    out_place = jnp.sum(jnp.where(pick_matrix, row_place[None, :] + 1, 0), axis=1) - 1
    place_cols = jnp.broadcast_to(out_place.astype(jnp.bfloat16)[:, None], (slot_count, 128))
    arrived = lax.all_to_all(
        jnp.concatenate([outgoing, place_cols], axis=1).reshape(dp_count, per_peer, feature_count + 128),
        "dp",
        split_axis=0,
        concat_axis=0,
        tiled=True,
    ).reshape(slot_count, feature_count + 128)
    arrived_place = arrived[:, feature_count].astype(jnp.int32)
    land_matrix = (
        arrived_place[None, :] == jnp.arange(shard_rows, dtype=jnp.int32)[:, None]
    ).astype(jnp.bfloat16)
    local_batch = jnp.dot(
        land_matrix, arrived[:, :feature_count], preferred_element_type=jnp.float32
    ).astype(jnp.bfloat16)

    ff_cols = gate_weight.shape[1]
    piece_rows = gate_weight.shape[0]
    buffers = gather_pieces(jnp.concatenate([gate_weight, up_weight], axis=1))
    keys = [k for ks, _ in buffers for k in ks]
    ny, nx, nc = DP_SUB
    me = lax.axis_index("dp")
    my_y, my_x, my_c = me // (nx * nc), (me // nc) % nx, me % nc
    piece_index = jnp.stack(
        [((my_y + k[0]) % ny) * nx * nc + ((my_x + k[1]) % nx) * nc + (my_c + k[2]) % nc for k in keys]
    ).astype(jnp.int32)

    nl, nz = TP_SUB
    travelling = normalize(local_batch)
    travelling = jnp.take(
        travelling.reshape(shard_rows, dp_count, piece_rows), piece_index, axis=1
    ).reshape(shard_rows, feature_count)
    pair = jnp.stack([travelling, lax.ppermute(travelling, "tensor", TP_L_SWAP)])
    token_chunks = {0: pair}
    fwd = pair
    for s in range(nz // 2 - 1):
        fwd = lax.ppermute(fwd, "tensor", TP_Z_FWD)
        token_chunks[nz - 1 - s] = fwd
    bwd = pair
    for s in range(nz // 2 - 1):
        bwd = lax.ppermute(bwd, "tensor", TP_Z_BWD)
        token_chunks[s + 1] = bwd
    half = feature_count // 2
    token_chunks[nz // 2] = jnp.concatenate(
        [
            lax.ppermute(fwd[..., :half], "tensor", TP_Z_FWD),
            lax.ppermute(bwd[..., half:], "tensor", TP_Z_BWD),
        ],
        axis=-1,
    )
    gathered = jnp.concatenate([token_chunks[k] for k in range(nz)], axis=0)
    row_total = gathered.shape[0] * gathered.shape[1]
    normed = gathered.reshape(row_total, feature_count)

    def ffn(rows):
        act = None
        col = 0
        for ks, buf in buffers:
            width = len(ks) * piece_rows
            part = jnp.dot(
                rows[:, col : col + width],
                buf.reshape(width, 2 * ff_cols),
                preferred_element_type=jnp.float32,
            )
            act = part if act is None else act + part
            col += width
        return (jax.nn.silu(act[:, :ff_cols]) * act[:, ff_cols:]).astype(jnp.bfloat16)

    def project(hidden):
        return jnp.dot(hidden, down_weight, preferred_element_type=jnp.float32).astype(jnp.bfloat16)

    chunk = nl * shard_rows
    blocks = {}
    groups = ([8, 9, 0, 1, 2, 3, 4, 5, 6, 7, 10, 11, 12, 13, 14, 15],)
    hiddens = [
        ffn(jnp.concatenate([normed[k * chunk : (k + 1) * chunk] for k in group], axis=0)) for group in groups
    ]

    def place(g, hidden):
        out = project(hidden).reshape(len(groups[g]), nl, shard_rows, feature_count)
        for i, k in enumerate(groups[g]):
            blocks[k] = out[i]

    place(0, hiddens[0])

    fwd = blocks[nz // 2]
    for s in range(nz // 2):
        if s == nz // 2 - 1:
            fwd_own = lax.ppermute(fwd[0], "tensor", TP_Z_FWD)
            fwd_diag = lax.ppermute(fwd[1], "tensor", TP_DIAG_FWD)
            break
        got = lax.ppermute(fwd, "tensor", TP_Z_FWD)
        if s < len(groups) - 1:
            late, got = lax.optimization_barrier((hiddens[s + 1], got))
            place(s + 1, late)
        fwd = (got.astype(jnp.float32) + blocks[nz // 2 - 1 - s].astype(jnp.float32)).astype(jnp.bfloat16)
    bwd = blocks[nz // 2 + 1]
    for s in range(nz // 2 - 1):
        got = lax.ppermute(bwd, "tensor", TP_Z_BWD)
        if s < nz // 2 - 2:
            bwd = (got.astype(jnp.float32) + blocks[nz // 2 + 2 + s].astype(jnp.float32)).astype(jnp.bfloat16)
        else:
            bwd_total = got
    f32 = lambda v: v.astype(jnp.float32)
    to_partner = (f32(bwd_total[1]) + f32(blocks[0][1])).astype(jnp.bfloat16)
    from_partner = lax.ppermute(to_partner, "tensor", TP_L_SWAP)
    total = f32(fwd_own) + f32(fwd_diag) + f32(bwd_total[0]) + f32(blocks[0][0]) + f32(from_partner)
    return (local_batch.astype(jnp.float32) + total).astype(jnp.bfloat16)


def solution(mesh):
    placed = (
        P("dp", "tensor", None, None),
        P("dp", "tensor"),
        P("dp", "tensor", None),
        P("dp", "tensor"),
        P("dp", "tensor"),
        P("tensor", None),
    )
    return jax.shard_map(
        per_device, mesh=mesh, in_specs=placed, out_specs=P(("dp", "tensor"), None), check_vma=False
    )
```

```python
import jax
import jax.numpy as jnp
from jax import lax
from jax.sharding import PartitionSpec as P

ROWS_GRP = 512
DP_SUB = (4, 2, 2)
TP_SUB = (2, 16)


def dp_perm(move):
    ny, nx, nc = DP_SUB
    pairs = []
    for y in range(ny):
        for x in range(nx):
            for c in range(nc):
                ty, tx, tc = move(y, x, c)
                pairs.append((y * nx * nc + x * nc + c, (ty % ny) * nx * nc + (tx % nx) * nc + tc % nc))
    return pairs


def tp_perm(move):
    nl, nz = TP_SUB
    pairs = []
    for l in range(nl):
        for z in range(nz):
            tl, tz = move(l, z)
            pairs.append((l * nz + z, (tl % nl) * nz + tz % nz))
    return pairs


DP_Y_FWD = dp_perm(lambda y, x, c: (y + 1, x, c))
DP_Y_BWD = dp_perm(lambda y, x, c: (y - 1, x, c))
DP_X_SWAP = dp_perm(lambda y, x, c: (y, x + 1, c))
DP_C_SWAP = dp_perm(lambda y, x, c: (y, x, c + 1))
TP_L_SWAP = tp_perm(lambda l, z: (l + 1, z))
TP_Z_FWD = tp_perm(lambda l, z: (l, z + 1))
TP_Z_BWD = tp_perm(lambda l, z: (l, z - 1))
TP_DIAG_FWD = tp_perm(lambda l, z: (l + 1, z + 1))


def normalize(row_block):
    wide_rows = row_block.astype(jnp.float32)
    return (
        wide_rows * lax.rsqrt(jnp.mean(wide_rows * wide_rows, axis=1, keepdims=True) + 1e-05)
    ).astype(jnp.bfloat16)


def gather_pieces(piece):
    ny = DP_SUB[0]
    own = piece[None]
    fwd1 = lax.ppermute(own, "dp", DP_Y_FWD)
    fwd2 = lax.ppermute(fwd1, "dp", DP_Y_FWD)
    bwd1 = lax.ppermute(own, "dp", DP_Y_BWD)
    col_keys = [(0, 0, 0), (ny - 1, 0, 0), (ny - 2, 0, 0), (1, 0, 0)]
    across = lax.ppermute(jnp.concatenate([own, fwd1, fwd2, bwd1]), "dp", DP_X_SWAP)
    across_keys = [(k[0], 1, 0) for k in col_keys]
    chip = jnp.concatenate([own, fwd1, fwd2, bwd1, across])
    other_core = lax.ppermute(chip, "dp", DP_C_SWAP)
    return [
        (col_keys[0:1], own),
        (col_keys[1:2], fwd1),
        (col_keys[2:3], fwd2),
        (col_keys[3:4], bwd1),
        (across_keys, across),
        ([(k[0], k[1], 1) for k in col_keys + across_keys], other_core),
    ]


def per_device(loader_rows, row_counts, row_targets, gate_weight, up_weight, down_weight):
    dp_count = lax.axis_size("dp")
    tp_count = lax.axis_size("tensor")
    slot_rows = loader_rows[0, 0]
    slot_targets = row_targets[0, 0]
    live_count = row_counts[0, 0]
    slot_count = slot_rows.shape[0]
    feature_count = slot_rows.shape[1]
    per_peer = slot_count // dp_count
    shard_rows = ROWS_GRP // tp_count
    slot_index = jnp.arange(slot_count, dtype=jnp.int32)
    is_live = slot_index < live_count
    peer_index = slot_targets // shard_rows
    row_place = slot_targets % shard_rows
    peer_hot = (
        (peer_index[:, None] == jnp.arange(dp_count, dtype=jnp.int32)[None, :]) & is_live[:, None]
    ).astype(jnp.int32)
    earlier = jnp.cumsum(peer_hot, axis=0) - peer_hot
    slot_rank = jnp.sum(earlier * peer_hot, axis=1)
    send_slot = peer_index * per_peer + slot_rank
    pick_matrix = (send_slot[None, :] == slot_index[:, None]) & is_live[None, :]
    outgoing = jnp.dot(
        pick_matrix.astype(jnp.bfloat16), slot_rows, preferred_element_type=jnp.float32
    ).astype(jnp.bfloat16)
    out_place = jnp.sum(jnp.where(pick_matrix, row_place[None, :] + 1, 0), axis=1) - 1
    place_cols = jnp.broadcast_to(out_place.astype(jnp.bfloat16)[:, None], (slot_count, 128))
    arrived = lax.all_to_all(
        jnp.concatenate([outgoing, place_cols], axis=1).reshape(dp_count, per_peer, feature_count + 128),
        "dp",
        split_axis=0,
        concat_axis=0,
        tiled=True,
    ).reshape(slot_count, feature_count + 128)
    arrived_place = arrived[:, feature_count].astype(jnp.int32)
    land_matrix = (
        arrived_place[None, :] == jnp.arange(shard_rows, dtype=jnp.int32)[:, None]
    ).astype(jnp.bfloat16)
    local_batch = jnp.dot(
        land_matrix, arrived[:, :feature_count], preferred_element_type=jnp.float32
    ).astype(jnp.bfloat16)

    ff_cols = gate_weight.shape[1]
    piece_rows = gate_weight.shape[0]
    buffers = gather_pieces(jnp.concatenate([gate_weight, up_weight], axis=1))
    keys = [k for ks, _ in buffers for k in ks]
    ny, nx, nc = DP_SUB
    me = lax.axis_index("dp")
    my_y, my_x, my_c = me // (nx * nc), (me // nc) % nx, me % nc
    piece_index = jnp.stack(
        [((my_y + k[0]) % ny) * nx * nc + ((my_x + k[1]) % nx) * nc + (my_c + k[2]) % nc for k in keys]
    ).astype(jnp.int32)

    nl, nz = TP_SUB
    travelling = normalize(local_batch)
    travelling = jnp.take(
        travelling.reshape(shard_rows, dp_count, piece_rows), piece_index, axis=1
    ).reshape(shard_rows, feature_count)
    pair = jnp.stack([travelling, lax.ppermute(travelling, "tensor", TP_L_SWAP)])
    token_chunks = {0: pair}
    fwd = pair
    for s in range(nz // 2 - 1):
        fwd = lax.ppermute(fwd, "tensor", TP_Z_FWD)
        token_chunks[nz - 1 - s] = fwd
    bwd = pair
    for s in range(nz // 2 - 1):
        bwd = lax.ppermute(bwd, "tensor", TP_Z_BWD)
        token_chunks[s + 1] = bwd
    half = feature_count // 2
    token_chunks[nz // 2] = jnp.concatenate(
        [
            lax.ppermute(fwd[..., :half], "tensor", TP_Z_FWD),
            lax.ppermute(bwd[..., half:], "tensor", TP_Z_BWD),
        ],
        axis=-1,
    )
    gathered = jnp.concatenate([token_chunks[k] for k in range(nz)], axis=0)
    row_total = gathered.shape[0] * gathered.shape[1]
    normed = gathered.reshape(row_total, feature_count)

    def ffn(rows):
        act = None
        col = 0
        for ks, buf in buffers:
            width = len(ks) * piece_rows
            part = jnp.dot(
                rows[:, col : col + width],
                buf.reshape(width, 2 * ff_cols),
                preferred_element_type=jnp.float32,
            )
            act = part if act is None else act + part
            col += width
        return (jax.nn.silu(act[:, :ff_cols]) * act[:, ff_cols:]).astype(jnp.bfloat16)

    def project(hidden):
        return jnp.dot(hidden, down_weight, preferred_element_type=jnp.float32).astype(jnp.bfloat16)

    chunk = nl * shard_rows
    blocks = {}
    groups = ([8, 9, 7, 10], [0, 1, 2, 3, 4, 5, 6, 11, 12, 13, 14, 15])
    hiddens = [
        ffn(jnp.concatenate([normed[k * chunk : (k + 1) * chunk] for k in group], axis=0)) for group in groups
    ]

    def place(g, hidden):
        out = project(hidden).reshape(len(groups[g]), nl, shard_rows, feature_count)
        for i, k in enumerate(groups[g]):
            blocks[k] = out[i]

    place(0, hiddens[0])

    fwd = blocks[nz // 2]
    for s in range(nz // 2):
        if s == nz // 2 - 1:
            fwd_own = lax.ppermute(fwd[0], "tensor", TP_Z_FWD)
            fwd_diag = lax.ppermute(fwd[1], "tensor", TP_DIAG_FWD)
            break
        got = lax.ppermute(fwd, "tensor", TP_Z_FWD)
        if s < len(groups) - 1:
            late, got = lax.optimization_barrier((hiddens[s + 1], got))
            place(s + 1, late)
        fwd = (got.astype(jnp.float32) + blocks[nz // 2 - 1 - s].astype(jnp.float32)).astype(jnp.bfloat16)
    bwd = blocks[nz // 2 + 1]
    for s in range(nz // 2 - 1):
        got = lax.ppermute(bwd, "tensor", TP_Z_BWD)
        if s < nz // 2 - 2:
            bwd = (got.astype(jnp.float32) + blocks[nz // 2 + 2 + s].astype(jnp.float32)).astype(jnp.bfloat16)
        else:
            bwd_total = got
    f32 = lambda v: v.astype(jnp.float32)
    to_partner = (f32(bwd_total[1]) + f32(blocks[0][1])).astype(jnp.bfloat16)
    from_partner = lax.ppermute(to_partner, "tensor", TP_L_SWAP)
    total = f32(fwd_own) + f32(fwd_diag) + f32(bwd_total[0]) + f32(blocks[0][0]) + f32(from_partner)
    return (local_batch.astype(jnp.float32) + total).astype(jnp.bfloat16)


def solution(mesh):
    placed = (
        P("dp", "tensor", None, None),
        P("dp", "tensor"),
        P("dp", "tensor", None),
        P("dp", "tensor"),
        P("dp", "tensor"),
        P("tensor", None),
    )
    return jax.shard_map(
        per_device, mesh=mesh, in_specs=placed, out_specs=P(("dp", "tensor"), None), check_vma=False
    )
```
